128 devices in a mesh: group: 8 (over z, core), member: 16 (over y, x).
Axes of the slice: x: 4, y: 4, z: 4, core: 2. Of those that a mesh axis runs over, the one named last changes fastest.
Arguments:
- embeddings: bfloat16 [65536, 1024], P(('group', 'member')), may hold values from -70 to 70
- coarse_ids: int32 [65536, 1], P(('group', 'member')), may hold values from 0 to 127; in each aligned block of 512 rows (0 to 511, 512 to 1023, ...) at most 8 rows name the same one
- centroid_seeds: bfloat16 [4096, 1024], P('group'), may hold values from -1 to 1
Outputs:
- refined_centroids: float32 [4096, 1024], P(('group', 'member'))
- row_energy: float32 [65536], P(('group', 'member'))
The draws below stay inside these ranges and needn't reach their ends.
Inputs may be any that keep to these rules, and one draw needn't show every extreme that they name: `coarse_ids`: in the rows of one device no coarse cluster is named by more than 8 rows.
All inputs are finite; a program needn't handle non-finite values.
Results may differ from the reference program's by a relative error of at most 0.00092.
Values may be sent and summed in bfloat16 or wider, within the bound.
No kernel may reach another device: no remote copies, remote signals or barrier semaphores. Data moves between devices by JAX's collectives and lax.ppermute only.
A program may use at most 64 MiB of HBM per device.

```python
import math
import jax
import jax.numpy as jnp
import numpy as np
from jax import lax

D = 1024
K = 512
ROWS_DEV = 512
ITERS = 2
CLUSTERS = 128
CAPC = 8
ROWS = 65536
CENTS = 4096
N_GROUP = 8
N_MEMBER = 16


def column_scales(key):
    return jnp.exp(jax.random.uniform(jax.random.fold_in(key, 3), (D,), jnp.float32, math.log(0.5), math.log(5.0)))


def prototype_pool(key):
    scales = column_scales(key)
    gaussian = jnp.clip(jax.random.normal(jax.random.fold_in(key, 21), (2 * K, D), jnp.float32), -4.0, 4.0)
    return gaussian * scales[None, :] / math.sqrt(5.37 * D)


def pick_subset(subkey):
    return jax.random.permutation(subkey, 2 * K)[:K]


def seed_choice(key):
    subkeys = jax.random.split(jax.random.fold_in(key, 23), CENTS // K)
    selected = jax.vmap(pick_subset)(subkeys)
    return selected.reshape(CENTS).astype(jnp.int32)


def cluster_pick(key):
    ceiling = jax.random.randint(jax.random.fold_in(key, 31), (ROWS,), 1, 2 * K + 1)
    return jax.random.randint(jax.random.fold_in(key, 32), (ROWS,), 0, ceiling)


def clustered_rows(key, deviation):
    prototypes = prototype_pool(key)
    chosen = prototypes[cluster_pick(key)]
    return 4.0 * (chosen + deviation)


def draw_embeddings(key, part):
    scales = column_scales(key)
    spread = scales[None, :] * (0.5 / math.sqrt(5.37 * D))
    clustered = jax.random.randint(jax.random.fold_in(key, 33), (ROWS, 1), 0, 20) < 17
    background = jnp.clip(jax.random.normal(jax.random.fold_in(key, 1), (ROWS, D), jnp.float32), -4.0, 4.0) * scales[None, :]
    deviation = jnp.clip(jax.random.normal(jax.random.fold_in(key, 8), (ROWS, D), jnp.float32), -4.0, 4.0) * spread
    values = jnp.where(clustered, clustered_rows(key, deviation), background)
    return jnp.clip(values, -69.0, 69.0).astype(jnp.bfloat16)


def draw_centroid_seeds(key, part):
    prototypes = prototype_pool(key)
    chosen = prototypes[seed_choice(key)]
    deviation = jnp.clip(jax.random.normal(jax.random.fold_in(key, 2), (CENTS, D), jnp.float32), -4.0, 4.0) * (0.3 / math.sqrt(D))
    values = chosen + deviation
    return jnp.clip(values, -1.0, 1.0).astype(jnp.bfloat16)


def assign_block(stream_key, own, number, rows, number_of, top, most, slope):
    ranking = jax.random.permutation(stream_key, number_of)
    packed, usual = load_shares(number_of, rows * top, most, slope, True), load_shares(number_of, rows * top, most, slope, False)
    places = jnp.arange(number_of)

    def named(tallies, rotation):
        used = int((tallies > 0).sum())
        fixed = max(1, used // 4)
        shifted = fixed + (places - fixed + rotation * (used - fixed)) % max(1, number_of - fixed)
        return jnp.zeros((number_of,), jnp.int32).at[ranking[jnp.where(places < fixed, places, shifted)]].set(jnp.asarray(tallies, jnp.int32))

    tallies = jnp.where(number % 4 == 0, named(packed, number // 4), named(usual, number - number // 4 - 1))
    mixed = jax.random.permutation(jax.random.fold_in(own, 3), number_of)
    donor, sink = mixed[0:number_of // 2 * 2:2], mixed[1:number_of // 2 * 2:2]
    room = jnp.minimum(tallies[donor] - 1, most - tallies[sink]) // 2
    room = jnp.where((donor == ranking[0]) | (sink == ranking[0]) | (tallies[sink] == 0), 0, jnp.maximum(room, 0))
    shifted = jax.random.randint(jax.random.fold_in(own, 4), (number_of // 2,), 0, 1 << 20) % (room + 1)
    tallies = tallies.at[donor].add(-shifted).at[sink].add(shifted)
    members = jnp.searchsorted(jnp.cumsum(tallies), jnp.arange(rows * top), side="right").astype(jnp.int32)
    grid = members.reshape(top, rows).T
    grid = grid[jax.random.permutation(jax.random.fold_in(own, 1), rows)]
    rotation = jax.random.randint(jax.random.fold_in(own, 2), (rows, 1), 0, top)
    return jnp.take_along_axis(grid, (jnp.arange(top)[None, :] + rotation) % top, axis=1)


def load_shares(count, total, reach, skew, full):
    portions = [(1 << 20) // math.isqrt(standing ** skew) + 1 for standing in range(1, count + 1)]
    largest = reach if full else min(reach, max(-(-total // count), total * portions[0] // sum(portions)))
    least = 1 if total - largest >= count - 1 else 0
    holding, spare = [largest] + [least] * (count - 1), total - largest - least * (count - 1)
    while spare > 0:
        candidates = [i for i in range(1, count) if holding[i] < largest] or [i for i in range(1, count) if holding[i] < reach]
        pool, budget = sum([portions[i] for i in candidates]), spare
        for i in candidates:
            more = min(reach - holding[i], max(1, budget * portions[i] // pool), spare)
            holding[i] = holding[i] + more
            spare = spare - more
    return np.array(holding)


def setup_inputs(seed: int = 0) -> dict:
    splits = jax.random.split(jax.random.key(seed), 4)
    embeddings = draw_embeddings(jax.random.fold_in(splits[3], 71), 0)
    coarse_ids_keys = jax.random.split(jax.random.fold_in(splits[1], 1), ROWS // ROWS_DEV)
    coarse_ids_turns = jax.random.permutation(jax.random.fold_in(splits[1], 3), ROWS // ROWS_DEV)
    coarse_ids = jax.vmap(lambda own, number: assign_block(jax.random.fold_in(splits[1], 2), own, number, ROWS_DEV, CLUSTERS, 1, CAPC, 2))(coarse_ids_keys, coarse_ids_turns).reshape((ROWS, 1))
    centroid_seeds = draw_centroid_seeds(jax.random.fold_in(splits[3], 71), 0)
    return dict(embeddings=embeddings, coarse_ids=coarse_ids, centroid_seeds=centroid_seeds)


smoothing_scale = 0.004
prior_mass = 32.0

def reference(embeddings, coarse_ids, centroid_seeds):
    widened = embeddings.astype(jnp.float32)
    unit_rows = (widened * lax.rsqrt(lax.optimization_barrier(jnp.mean(widened * widened, axis=1, keepdims=True)) + 1e-06) / math.sqrt(D)).astype(jnp.bfloat16)
    owner_range = (coarse_ids[:, 0] // N_MEMBER).astype(jnp.int32)
    grouping_maximal_logit = 2 * ROWS // N_GROUP
    block_rows = 2 * ROWS_DEV
    block_count = grouping_maximal_logit // block_rows

    def one_group(energy_acc, group_id):
        keyed = jnp.where(owner_range == group_id, 0, 1).astype(jnp.int32)
        ordering = jnp.argsort(keyed, stable=True)[:grouping_maximal_logit].astype(jnp.int32)
        legitimate_indicator = (owner_range[ordering] == group_id).astype(jnp.float32)
        group_rows = unit_rows[ordering].reshape(block_count, block_rows, D)
        valid_blocks = legitimate_indicator.reshape(block_count, block_rows)
        start = (group_id * K).astype(jnp.int32)
        centroids = lax.dynamic_slice_in_dim(centroid_seeds, start, K, 0).astype(jnp.float32)
        closing_log_partition = jnp.zeros((block_count, block_rows), jnp.float32)
        for iteration in range(ITERS):
            prototype_lowbits = centroids.astype(jnp.bfloat16)
            half_quadratic_length = 0.5 * lax.optimization_barrier(jnp.sum(centroids * centroids, axis=1))

            def block_pass(carry, inputs):
                weighted, masses = carry
                tile_vectors, valid_blk = inputs
                similarity_logits = (jnp.dot(tile_vectors, prototype_lowbits.T, preferred_element_type=jnp.float32) - half_quadratic_length[None, :]) / smoothing_scale
                row_max = lax.optimization_barrier(jnp.max(similarity_logits, axis=1, keepdims=True))
                powers = jnp.exp(similarity_logits - row_max)
                row_sum = lax.optimization_barrier(jnp.sum(powers, axis=1, keepdims=True))
                weights = (powers / row_sum * valid_blk[:, None]).astype(jnp.bfloat16)
                weighted = weighted + jnp.dot(weights.T, tile_vectors, preferred_element_type=jnp.float32)
                masses = masses + lax.optimization_barrier(jnp.sum(weights.astype(jnp.float32), axis=0))
                lse = row_max[:, 0] + jnp.log(row_sum[:, 0])
                return ((weighted, masses), lse)
            init = (jnp.zeros((K, D), jnp.float32), jnp.zeros((K,), jnp.float32))
            (weighted, masses), closing_log_partition = lax.scan(block_pass, init, (group_rows, valid_blocks))
            centroids = (weighted + prior_mass * centroids) / (masses + prior_mass)[:, None]
        incomplete_summand = jnp.where(legitimate_indicator > 0.5, smoothing_scale * closing_log_partition.reshape(grouping_maximal_logit), 0.0)
        energy_acc = energy_acc.at[ordering].add(incomplete_summand)
        return (energy_acc, centroids)
    energy, all_cents = lax.scan(one_group, jnp.zeros((ROWS,), jnp.float32), jnp.arange(N_GROUP, dtype=jnp.int32))
    return (all_cents.reshape(N_GROUP * K, D), energy)
```

```python
import math

import jax
import jax.numpy as jnp
from jax import lax
from jax.sharding import PartitionSpec as P

K = 512
ITERS = 2


smoothing_scale = 0.004
prior_mass = 32.0
empty_mark = 2.0


def shards(embeddings, coarse_ids, centroid_seeds):
    rows_dev, features = embeddings.shape
    groups = lax.axis_size("group")
    members = lax.axis_size("member")
    clusters = groups * members
    capacity = 2 * rows_dev // clusters
    share_rows = K // members
    first_row = lax.axis_index("member") * share_rows
    widened = embeddings.astype(jnp.float32)
    unit_rows = (
        widened
        * lax.rsqrt(jnp.mean(widened * widened, axis=1, keepdims=True) + 1e-06)
        / math.sqrt(features)
    ).astype(jnp.bfloat16)
    cluster_of = coarse_ids[:, 0]
    onehot = (cluster_of[:, None] == jnp.arange(clusters, dtype=jnp.int32)[None, :]).astype(
        jnp.int32
    )
    row_rank = jnp.sum((jnp.cumsum(onehot, axis=0) - onehot) * onehot, axis=1)
    slot_of = cluster_of * capacity + row_rank
    source = (
        jnp.full((clusters * capacity,), -1, jnp.int32)
        .at[slot_of]
        .set(jnp.arange(rows_dev, dtype=jnp.int32))
    )
    filled = source >= 0
    empty_row = jnp.where(
        jnp.arange(features) == 0, jnp.bfloat16(empty_mark), jnp.bfloat16(0)
    ).astype(jnp.bfloat16)
    packed = jnp.where(filled[:, None], unit_rows[jnp.maximum(source, 0)], empty_row[None, :])
    arrived = lax.all_to_all(packed, ("group", "member"), split_axis=0, concat_axis=0, tiled=True)
    slot_mask = (arrived[:, 0].astype(jnp.float32) < 1.5).astype(jnp.float32)
    seeds = centroid_seeds.astype(jnp.float32)
    own = lax.dynamic_slice_in_dim(seeds, first_row, share_rows, 0)
    prototype_lowbits = centroid_seeds
    half_quadratic_length = 0.5 * jnp.sum(seeds * seeds, axis=1)
    closing_log_partition = jnp.zeros((clusters * capacity,), jnp.float32)
    for iteration in range(ITERS):
        similarity_logits = (
            jnp.dot(arrived, prototype_lowbits.T, preferred_element_type=jnp.float32)
            - half_quadratic_length[None, :]
        ) / smoothing_scale
        row_max = jnp.max(similarity_logits, axis=1, keepdims=True)
        powers = jnp.exp(similarity_logits - row_max)
        row_sum = jnp.sum(powers, axis=1, keepdims=True)
        weights = (powers / row_sum * slot_mask[:, None]).astype(jnp.bfloat16)
        closing_log_partition = row_max[:, 0] + jnp.log(row_sum[:, 0])
        weighted = jnp.einsum("rk,rd->kd", weights, arrived, preferred_element_type=jnp.float32)
        masses = jnp.sum(weights.astype(jnp.float32), axis=0)
        combined = jnp.concatenate(
            [
                weighted.reshape(members, share_rows * features),
                jnp.pad(masses.reshape(members, share_rows), ((0, 0), (0, 128 - share_rows))),
            ],
            axis=1,
        )
        reduced = jnp.sum(
            lax.all_to_all(combined, "member", split_axis=0, concat_axis=0, tiled=True),
            axis=0,
            keepdims=True,
        )
        weighted_own = reduced[0, : share_rows * features].reshape(share_rows, features)
        masses_own = reduced[0, share_rows * features : share_rows * features + share_rows]
        own = (weighted_own + prior_mass * own) / (masses_own + prior_mass)[:, None]
        if iteration + 1 < ITERS:
            prototype_lowbits = lax.all_gather(
                own.astype(jnp.bfloat16), "member", axis=0, tiled=True
            )
            half_quadratic_length = lax.all_gather(
                0.5 * jnp.sum(own * own, axis=1), "member", axis=0, tiled=True
            )
    prototype_position_cost = smoothing_scale * closing_log_partition
    returned = lax.all_to_all(
        prototype_position_cost, ("group", "member"), split_axis=0, concat_axis=0, tiled=True
    )
    row_energy = returned[slot_of]
    return (own, row_energy)


def solution(mesh):
    in_specs = (P(("group", "member"), None), P(("group", "member"), None), P("group", None))
    out_specs = (P(("group", "member"), None), P(("group", "member")))
    return jax.shard_map(shards, mesh=mesh, in_specs=in_specs, out_specs=out_specs, check_vma=False)
```

```python
import math

import jax
import jax.numpy as jnp
from jax import lax
from jax.sharding import PartitionSpec as P

K = 512
ITERS = 2


smoothing_scale = 0.004
prior_mass = 32.0
empty_mark = 2.0


def shards(embeddings, coarse_ids, centroid_seeds):
    rows_dev, features = embeddings.shape
    groups = lax.axis_size("group")
    members = lax.axis_size("member")
    clusters = groups * members
    capacity = 2 * rows_dev // clusters
    share_rows = K // members
    first_row = lax.axis_index("member") * share_rows
    widened = embeddings.astype(jnp.float32)
    unit_rows = (
        widened
        * lax.rsqrt(jnp.mean(widened * widened, axis=1, keepdims=True) + 1e-06)
        / math.sqrt(features)
    ).astype(jnp.bfloat16)
    cluster_of = coarse_ids[:, 0]
    onehot = (cluster_of[:, None] == jnp.arange(clusters, dtype=jnp.int32)[None, :]).astype(
        jnp.int32
    )
    row_rank = jnp.sum((jnp.cumsum(onehot, axis=0) - onehot) * onehot, axis=1)
    slot_of = cluster_of * capacity + row_rank
    placement = (
        slot_of[None, :] == jnp.arange(clusters * capacity, dtype=jnp.int32)[:, None]
    ).astype(jnp.bfloat16)
    filled = jnp.sum(placement.astype(jnp.float32), axis=1) > 0.5
    empty_row = jnp.where(
        jnp.arange(features) == 0, jnp.bfloat16(empty_mark), jnp.bfloat16(0)
    ).astype(jnp.bfloat16)
    gathered = jnp.dot(placement, unit_rows, preferred_element_type=jnp.float32).astype(
        jnp.bfloat16
    )
    packed = jnp.where(filled[:, None], gathered, empty_row[None, :])
    arrived = lax.all_to_all(packed, ("group", "member"), split_axis=0, concat_axis=0, tiled=True)
    slot_mask = (arrived[:, 0].astype(jnp.float32) < 1.5).astype(jnp.float32)
    seeds = centroid_seeds.astype(jnp.float32)
    own = lax.dynamic_slice_in_dim(seeds, first_row, share_rows, 0)
    prototype_lowbits = centroid_seeds
    half_quadratic_length = 0.5 * jnp.sum(seeds * seeds, axis=1)
    closing_log_partition = jnp.zeros((clusters * capacity,), jnp.float32)
    for iteration in range(ITERS):
        similarity_logits = (
            jnp.dot(arrived, prototype_lowbits.T, preferred_element_type=jnp.float32)
            - half_quadratic_length[None, :]
        ) / smoothing_scale
        row_max = jnp.max(similarity_logits, axis=1, keepdims=True)
        powers = jnp.exp(similarity_logits - row_max)
        row_sum = jnp.sum(powers, axis=1, keepdims=True)
        weights = (powers / row_sum * slot_mask[:, None]).astype(jnp.bfloat16)
        closing_log_partition = row_max[:, 0] + jnp.log(row_sum[:, 0])
        weighted = jnp.einsum("rk,rd->kd", weights, arrived, preferred_element_type=jnp.float32)
        masses = jnp.sum(weights.astype(jnp.float32), axis=0)
        combined = jnp.concatenate(
            [
                weighted.reshape(members, share_rows * features),
                jnp.pad(masses.reshape(members, share_rows), ((0, 0), (0, 128 - share_rows))),
            ],
            axis=1,
        )
        reduced = jnp.sum(
            lax.all_to_all(combined, "member", split_axis=0, concat_axis=0, tiled=True),
            axis=0,
            keepdims=True,
        )
        weighted_own = reduced[0, : share_rows * features].reshape(share_rows, features)
        masses_own = reduced[0, share_rows * features : share_rows * features + share_rows]
        own = (weighted_own + prior_mass * own) / (masses_own + prior_mass)[:, None]
        if iteration + 1 < ITERS:
            half_own = 0.5 * jnp.sum(own * own, axis=1)
            high = lax.reduce_precision(half_own, exponent_bits=8, mantissa_bits=7)
            rest = half_own - high
            middle = lax.reduce_precision(rest, exponent_bits=8, mantissa_bits=7)
            low = rest - middle
            block = jnp.concatenate(
                [
                    own.astype(jnp.bfloat16),
                    jnp.stack([high, middle, low], axis=1).astype(jnp.bfloat16),
                    jnp.zeros((share_rows, 125), jnp.bfloat16),
                ],
                axis=1,
            )
            everyone = lax.all_to_all(
                jnp.broadcast_to(block[None], (members,) + block.shape),
                "member",
                split_axis=0,
                concat_axis=0,
                tiled=True,
            ).reshape(K, features + 128)
            prototype_lowbits = everyone[:, :features]
            parts = everyone[:, features : features + 3].astype(jnp.float32)
            half_quadratic_length = (parts[:, 0] + parts[:, 1]) + parts[:, 2]
    prototype_position_cost = smoothing_scale * closing_log_partition
    returned = lax.all_to_all(
        prototype_position_cost, ("group", "member"), split_axis=0, concat_axis=0, tiled=True
    )
    row_energy = returned[slot_of]
    return (own, row_energy)


def solution(mesh):
    in_specs = (P(("group", "member"), None), P(("group", "member"), None), P("group", None))
    out_specs = (P(("group", "member"), None), P(("group", "member")))
    return jax.shard_map(shards, mesh=mesh, in_specs=in_specs, out_specs=out_specs, check_vma=False)
```

```python
import math

import jax
import jax.numpy as jnp
from jax import lax
from jax.sharding import PartitionSpec as P

K = 512
ITERS = 2


smoothing_scale = 0.004
prior_mass = 32.0
empty_mark = 2.0


def shards(embeddings, coarse_ids, centroid_seeds):
    rows_dev, features = embeddings.shape
    groups = lax.axis_size("group")
    members = lax.axis_size("member")
    clusters = groups * members
    capacity = 2 * rows_dev // clusters
    share_rows = K // members
    first_row = lax.axis_index("member") * share_rows
    widened = embeddings.astype(jnp.float32)
    unit_rows = (
        widened
        * lax.rsqrt(jnp.mean(widened * widened, axis=1, keepdims=True) + 1e-06)
        / math.sqrt(features)
    ).astype(jnp.bfloat16)
    cluster_of = coarse_ids[:, 0]
    onehot = (cluster_of[:, None] == jnp.arange(clusters, dtype=jnp.int32)[None, :]).astype(
        jnp.int32
    )
    row_rank = jnp.sum((jnp.cumsum(onehot, axis=0) - onehot) * onehot, axis=1)
    slot_of = cluster_of * capacity + row_rank
    placement = (
        slot_of[None, :] == jnp.arange(clusters * capacity, dtype=jnp.int32)[:, None]
    ).astype(jnp.bfloat16)
    filled = jnp.sum(placement.astype(jnp.float32), axis=1) > 0.5
    empty_row = jnp.where(
        jnp.arange(features) == 0, jnp.bfloat16(empty_mark), jnp.bfloat16(0)
    ).astype(jnp.bfloat16)
    gathered = jnp.dot(placement, unit_rows, preferred_element_type=jnp.float32).astype(
        jnp.bfloat16
    )
    packed = jnp.where(filled[:, None], gathered, empty_row[None, :])
    arrived = lax.all_to_all(packed, ("group", "member"), split_axis=0, concat_axis=0, tiled=True)
    slot_mask = (arrived[:, 0].astype(jnp.float32) < 1.5).astype(jnp.float32)
    seeds = centroid_seeds.astype(jnp.float32)
    own = lax.dynamic_slice_in_dim(seeds, first_row, share_rows, 0)
    prototype_lowbits = centroid_seeds
    half_quadratic_length = 0.5 * jnp.sum(seeds * seeds, axis=1)
    closing_log_partition = jnp.zeros((clusters * capacity,), jnp.float32)
    for iteration in range(ITERS):
        similarity_logits = (
            jnp.dot(arrived, prototype_lowbits.T, preferred_element_type=jnp.float32)
            - half_quadratic_length[None, :]
        ) / smoothing_scale
        row_max = jnp.max(similarity_logits, axis=1, keepdims=True)
        powers = jnp.exp(similarity_logits - row_max)
        row_sum = jnp.sum(powers, axis=1, keepdims=True)
        weights = (powers / row_sum * slot_mask[:, None]).astype(jnp.bfloat16)
        closing_log_partition = row_max[:, 0] + jnp.log(row_sum[:, 0])
        weighted = jnp.einsum("rk,rd->kd", weights, arrived, preferred_element_type=jnp.float32)
        masses = jnp.sum(weights.astype(jnp.float32), axis=0)
        combined = jnp.concatenate(
            [weighted, masses[:, None], jnp.zeros((K, 127), jnp.float32)], axis=1
        ).reshape(members, share_rows, features + 128)
        reduced = jnp.sum(
            lax.all_to_all(combined, "member", split_axis=0, concat_axis=0, tiled=True), axis=0
        )
        weighted_own = reduced[:, :features]
        masses_own = reduced[:, features]
        own = (weighted_own + prior_mass * own) / (masses_own + prior_mass)[:, None]
        if iteration + 1 < ITERS:
            half_own = 0.5 * jnp.sum(own * own, axis=1)
            high = lax.reduce_precision(half_own, exponent_bits=8, mantissa_bits=7)
            rest = half_own - high
            middle = lax.reduce_precision(rest, exponent_bits=8, mantissa_bits=7)
            low = rest - middle
            block = jnp.concatenate(
                [
                    own.astype(jnp.bfloat16),
                    jnp.stack([high, middle, low], axis=1).astype(jnp.bfloat16),
                    jnp.zeros((share_rows, 125), jnp.bfloat16),
                ],
                axis=1,
            )
            everyone = lax.all_to_all(
                jnp.broadcast_to(block[None], (members,) + block.shape),
                "member",
                split_axis=0,
                concat_axis=0,
                tiled=True,
            ).reshape(K, features + 128)
            prototype_lowbits = everyone[:, :features]
            parts = everyone[:, features : features + 3].astype(jnp.float32)
            half_quadratic_length = (parts[:, 0] + parts[:, 1]) + parts[:, 2]
    prototype_position_cost = smoothing_scale * closing_log_partition
    returned = lax.all_to_all(
        prototype_position_cost, ("group", "member"), split_axis=0, concat_axis=0, tiled=True
    )
    row_energy = returned[slot_of]
    return (own, row_energy)


def solution(mesh):
    in_specs = (P(("group", "member"), None), P(("group", "member"), None), P("group", None))
    out_specs = (P(("group", "member"), None), P(("group", "member")))
    return jax.shard_map(shards, mesh=mesh, in_specs=in_specs, out_specs=out_specs, check_vma=False)
```

```python
import math

import jax
import jax.numpy as jnp
from jax import lax
from jax.sharding import Mesh
from jax.sharding import PartitionSpec as P

K = 512
ITERS = 2


smoothing_scale = 0.004
prior_mass = 32.0
empty_mark = 2.0

ALL = ("z", "core", "yhi", "ylo", "x")
ROUTE = ("z", "yhi", "core", "ylo", "x")
TEAM = ("core", "ylo", "x")
PLANE = ("ylo", "x")


def shards(embeddings, coarse_ids, centroid_seeds):
    rows_dev, features = embeddings.shape
    cores = lax.axis_size("core")
    plane = lax.axis_size("ylo") * lax.axis_size("x")
    members = cores * plane
    clusters = members * lax.axis_size("z") * lax.axis_size("yhi")
    capacity = 2 * rows_dev // clusters
    share_rows = K // members
    core = lax.axis_index("core")
    yhi = lax.axis_index("yhi")
    first_row = lax.axis_index(TEAM) * share_rows
    partner = lax.ppermute(centroid_seeds, "core", [(0, 1), (1, 0)])
    seeds16 = jnp.where(core == yhi, centroid_seeds, partner)
    widened = embeddings.astype(jnp.float32)
    unit_rows = (
        widened
        * lax.rsqrt(jnp.mean(widened * widened, axis=1, keepdims=True) + 1e-06)
        / math.sqrt(features)
    ).astype(jnp.bfloat16)
    cluster_of = coarse_ids[:, 0]
    onehot = (cluster_of[:, None] == jnp.arange(clusters, dtype=jnp.int32)[None, :]).astype(
        jnp.int32
    )
    row_rank = jnp.sum((jnp.cumsum(onehot, axis=0) - onehot) * onehot, axis=1)
    slot_of = cluster_of * capacity + row_rank
    placement = (
        slot_of[None, :] == jnp.arange(clusters * capacity, dtype=jnp.int32)[:, None]
    ).astype(jnp.bfloat16)
    filled = jnp.sum(placement.astype(jnp.float32), axis=1) > 0.5
    empty_row = jnp.where(
        jnp.arange(features) == 0, jnp.bfloat16(empty_mark), jnp.bfloat16(0)
    ).astype(jnp.bfloat16)
    gathered = jnp.dot(placement, unit_rows, preferred_element_type=jnp.float32).astype(
        jnp.bfloat16
    )
    packed = jnp.where(filled[:, None], gathered, empty_row[None, :])
    arrived = lax.all_to_all(packed, ROUTE, split_axis=0, concat_axis=0, tiled=True)
    slot_mask = (arrived[:, 0].astype(jnp.float32) < 1.5).astype(jnp.float32)
    seeds = seeds16.astype(jnp.float32)
    own = lax.dynamic_slice_in_dim(seeds, first_row, share_rows, 0)
    prototype_lowbits = seeds16
    half_quadratic_length = 0.5 * jnp.sum(seeds * seeds, axis=1)
    closing_log_partition = jnp.zeros((clusters * capacity,), jnp.float32)
    for iteration in range(ITERS):
        similarity_logits = (
            jnp.dot(arrived, prototype_lowbits.T, preferred_element_type=jnp.float32)
            - half_quadratic_length[None, :]
        ) / smoothing_scale
        row_max = jnp.max(similarity_logits, axis=1, keepdims=True)
        powers = jnp.exp(similarity_logits - row_max)
        row_sum = jnp.sum(powers, axis=1, keepdims=True)
        weights = (powers / row_sum * slot_mask[:, None]).astype(jnp.bfloat16)
        closing_log_partition = row_max[:, 0] + jnp.log(row_sum[:, 0])
        weighted = jnp.einsum("rk,rd->kd", weights, arrived, preferred_element_type=jnp.float32)
        masses = jnp.sum(weights.astype(jnp.float32), axis=0)
        combined = jnp.concatenate(
            [
                weighted.reshape(members, share_rows * features),
                jnp.pad(masses.reshape(members, share_rows), ((0, 0), (0, 128 - share_rows))),
            ],
            axis=1,
        )
        width = combined.shape[1]
        halves = jnp.sum(
            lax.all_to_all(
                combined.reshape(cores, plane, width), "core", split_axis=0, concat_axis=0,
                tiled=True,
            ),
            axis=0,
        )
        reduced = jnp.sum(
            lax.all_to_all(halves, PLANE, split_axis=0, concat_axis=0, tiled=True),
            axis=0,
            keepdims=True,
        )
        weighted_own = reduced[0, : share_rows * features].reshape(share_rows, features)
        masses_own = reduced[0, share_rows * features : share_rows * features + share_rows]
        own = (weighted_own + prior_mass * own) / (masses_own + prior_mass)[:, None]
        if iteration + 1 < ITERS:
            half_own = 0.5 * jnp.sum(own * own, axis=1)
            high = lax.reduce_precision(half_own, exponent_bits=8, mantissa_bits=7)
            rest = half_own - high
            middle = lax.reduce_precision(rest, exponent_bits=8, mantissa_bits=7)
            low = rest - middle
            block = jnp.concatenate(
                [
                    own.astype(jnp.bfloat16),
                    jnp.stack([high, middle, low], axis=1).astype(jnp.bfloat16),
                    jnp.zeros((share_rows, 125), jnp.bfloat16),
                ],
                axis=1,
            )
            on_plane = lax.all_to_all(
                jnp.broadcast_to(block[None], (plane,) + block.shape),
                PLANE,
                split_axis=0,
                concat_axis=0,
                tiled=True,
            )
            everyone = lax.all_to_all(
                jnp.broadcast_to(on_plane[None], (cores,) + on_plane.shape),
                "core",
                split_axis=0,
                concat_axis=0,
                tiled=True,
            ).reshape(K, features + 128)
            prototype_lowbits = everyone[:, :features]
            parts = everyone[:, features : features + 3].astype(jnp.float32)
            half_quadratic_length = (parts[:, 0] + parts[:, 1]) + parts[:, 2]
    prototype_position_cost = smoothing_scale * closing_log_partition
    returned = lax.all_to_all(
        prototype_position_cost, ROUTE, split_axis=0, concat_axis=0, tiled=True
    )
    row_energy = returned[slot_of]
    refined = lax.ppermute(own, ("core", "yhi"), [(0, 0), (1, 2), (2, 1), (3, 3)])
    return (refined, row_energy)


def solution(mesh):
    groups, members = mesh.devices.shape
    fine = Mesh(mesh.devices.reshape(groups // 2, 2, 2, members // 8, 4), ALL)
    in_specs = (P(ALL, None), P(ALL, None), P(("z", "core"), None))
    out_specs = (P(ALL, None), P(ALL))
    return jax.shard_map(shards, mesh=fine, in_specs=in_specs, out_specs=out_specs, check_vma=False)
```

```python
import math

import jax
import jax.numpy as jnp
from jax import lax
from jax.sharding import Mesh
from jax.sharding import PartitionSpec as P

K = 512
ITERS = 2


smoothing_scale = 0.004
prior_mass = 32.0
empty_mark = 2.0

ALL = ("z", "core", "yhi", "ylo", "x")
ROUTE = ("z", "yhi", "core", "ylo", "x")
TEAM = ("core", "ylo", "x")
PLANE = ("ylo", "x")


def shards(embeddings, coarse_ids, centroid_seeds):
    rows_dev, features = embeddings.shape
    cores = lax.axis_size("core")
    plane = lax.axis_size("ylo") * lax.axis_size("x")
    members = cores * plane
    clusters = members * lax.axis_size("z") * lax.axis_size("yhi")
    capacity = 2 * rows_dev // clusters
    share_rows = K // members
    core = lax.axis_index("core")
    yhi = lax.axis_index("yhi")
    first_row = lax.axis_index(TEAM) * share_rows
    partner = lax.ppermute(centroid_seeds, "core", [(0, 1), (1, 0)])
    seeds16 = jnp.where(core == yhi, centroid_seeds, partner)
    widened = embeddings.astype(jnp.float32)
    unit_rows = (
        widened
        * lax.rsqrt(jnp.mean(widened * widened, axis=1, keepdims=True) + 1e-06)
        / math.sqrt(features)
    ).astype(jnp.bfloat16)
    cluster_of = coarse_ids[:, 0]
    onehot = (cluster_of[:, None] == jnp.arange(clusters, dtype=jnp.int32)[None, :]).astype(
        jnp.int32
    )
    row_rank = jnp.sum((jnp.cumsum(onehot, axis=0) - onehot) * onehot, axis=1)
    slot_of = cluster_of * capacity + row_rank
    placement = (
        slot_of[None, :] == jnp.arange(clusters * capacity, dtype=jnp.int32)[:, None]
    ).astype(jnp.bfloat16)
    filled = jnp.sum(placement.astype(jnp.float32), axis=1) > 0.5
    empty_row = jnp.where(
        jnp.arange(features) == 0, jnp.bfloat16(empty_mark), jnp.bfloat16(0)
    ).astype(jnp.bfloat16)
    gathered = jnp.dot(placement, unit_rows, preferred_element_type=jnp.float32).astype(
        jnp.bfloat16
    )
    packed = jnp.where(filled[:, None], gathered, empty_row[None, :])
    arrived = lax.all_to_all(packed, ROUTE, split_axis=0, concat_axis=0, tiled=True)
    slot_mask = (arrived[:, 0].astype(jnp.float32) < 1.5).astype(jnp.float32)
    seeds = seeds16.astype(jnp.float32)
    own = lax.dynamic_slice_in_dim(seeds, first_row, share_rows, 0)
    prototype_lowbits = seeds16
    half_quadratic_length = 0.5 * jnp.sum(seeds * seeds, axis=1)
    for iteration in range(ITERS):
        similarity_logits = (
            jnp.dot(arrived, prototype_lowbits.T, preferred_element_type=jnp.float32)
            - half_quadratic_length[None, :]
        ) / smoothing_scale
        row_max = jnp.max(similarity_logits, axis=1, keepdims=True)
        powers = jnp.exp(similarity_logits - row_max)
        row_sum = jnp.sum(powers, axis=1, keepdims=True)
        weights = (powers / row_sum * slot_mask[:, None]).astype(jnp.bfloat16)
        closing_log_partition = row_max[:, 0] + jnp.log(row_sum[:, 0])
        if iteration + 1 == ITERS:
            returned = lax.all_to_all(
                smoothing_scale * closing_log_partition, ROUTE, split_axis=0, concat_axis=0,
                tiled=True,
            )
        weighted = jnp.einsum("rk,rd->kd", weights, arrived, preferred_element_type=jnp.float32)
        masses = jnp.sum(weights.astype(jnp.float32), axis=0)
        combined = jnp.concatenate(
            [
                weighted.reshape(members, share_rows * features),
                jnp.pad(masses.reshape(members, share_rows), ((0, 0), (0, 128 - share_rows))),
            ],
            axis=1,
        )
        width = combined.shape[1]
        by_core = combined.reshape(cores, plane, width)
        mine = lax.dynamic_index_in_dim(by_core, core, 0, keepdims=False)
        theirs = lax.dynamic_index_in_dim(by_core, 1 - core, 0, keepdims=False)
        halves = mine + lax.ppermute(theirs, "core", [(0, 1), (1, 0)])
        if iteration + 1 == ITERS:
            returned, halves = lax.optimization_barrier((returned, halves))
        reduced = jnp.sum(
            lax.all_to_all(halves, PLANE, split_axis=0, concat_axis=0, tiled=True),
            axis=0,
            keepdims=True,
        )
        weighted_own = reduced[0, : share_rows * features].reshape(share_rows, features)
        masses_own = reduced[0, share_rows * features : share_rows * features + share_rows]
        own = (weighted_own + prior_mass * own) / (masses_own + prior_mass)[:, None]
        if iteration + 1 < ITERS:
            half_own = 0.5 * jnp.sum(own * own, axis=1)
            high = lax.reduce_precision(half_own, exponent_bits=8, mantissa_bits=7)
            rest = half_own - high
            middle = lax.reduce_precision(rest, exponent_bits=8, mantissa_bits=7)
            low = rest - middle
            block = jnp.concatenate(
                [
                    own.astype(jnp.bfloat16),
                    jnp.stack([high, middle, low], axis=1).astype(jnp.bfloat16),
                    jnp.zeros((share_rows, 125), jnp.bfloat16),
                ],
                axis=1,
            )
            on_plane = lax.all_to_all(
                jnp.broadcast_to(block[None], (plane,) + block.shape),
                PLANE,
                split_axis=0,
                concat_axis=0,
                tiled=True,
            )
            partner_plane = lax.ppermute(on_plane, "core", [(0, 1), (1, 0)])
            everyone = jnp.concatenate(
                [
                    jnp.where(core == 0, on_plane, partner_plane),
                    jnp.where(core == 0, partner_plane, on_plane),
                ],
                axis=0,
            ).reshape(K, features + 128)
            prototype_lowbits = everyone[:, :features]
            parts = everyone[:, features : features + 3].astype(jnp.float32)
            half_quadratic_length = (parts[:, 0] + parts[:, 1]) + parts[:, 2]
    own_slot = slot_of[None, :] == jnp.arange(clusters * capacity, dtype=jnp.int32)[:, None]
    row_energy = jnp.sum(jnp.where(own_slot, returned[:, None], 0.0), axis=0)
    refined = lax.ppermute(own, ("core", "yhi"), [(0, 0), (1, 2), (2, 1), (3, 3)])
    return (refined, row_energy)


def solution(mesh):
    groups, members = mesh.devices.shape
    fine = Mesh(mesh.devices.reshape(groups // 2, 2, 2, members // 8, 4), ALL)
    in_specs = (P(ALL, None), P(ALL, None), P(("z", "core"), None))
    out_specs = (P(ALL, None), P(ALL))
    return jax.shard_map(shards, mesh=fine, in_specs=in_specs, out_specs=out_specs, check_vma=False)
```

```python
import math

import jax
import jax.numpy as jnp
from jax import lax
from jax.sharding import Mesh
from jax.sharding import PartitionSpec as P

K = 512
ITERS = 2


smoothing_scale = 0.004
prior_mass = 32.0
empty_mark = 2.0

ALL = ("z", "core", "yhi", "ylo", "x")
ROUTE = ("z", "yhi", "core", "ylo", "x")
TEAM = ("core", "ylo", "x")
PLANE = ("ylo", "x")


def shards(embeddings, coarse_ids, centroid_seeds):
    rows_dev, features = embeddings.shape
    cores = lax.axis_size("core")
    plane = lax.axis_size("ylo") * lax.axis_size("x")
    members = cores * plane
    clusters = members * lax.axis_size("z") * lax.axis_size("yhi")
    capacity = 2 * rows_dev // clusters
    share_rows = K // members
    core = lax.axis_index("core")
    yhi = lax.axis_index("yhi")
    first_row = lax.axis_index(TEAM) * share_rows
    partner = lax.ppermute(centroid_seeds, "core", [(0, 1), (1, 0)])
    seeds16 = jnp.where(core == yhi, centroid_seeds, partner)
    widened = embeddings.astype(jnp.float32)
    unit_rows = (
        widened
        * lax.rsqrt(jnp.mean(widened * widened, axis=1, keepdims=True) + 1e-06)
        / math.sqrt(features)
    ).astype(jnp.bfloat16)
    cluster_of = coarse_ids[:, 0]
    onehot = (cluster_of[:, None] == jnp.arange(clusters, dtype=jnp.int32)[None, :]).astype(
        jnp.int32
    )
    row_rank = jnp.sum((jnp.cumsum(onehot, axis=0) - onehot) * onehot, axis=1)
    slot_of = cluster_of * capacity + row_rank
    placement = (
        slot_of[None, :] == jnp.arange(clusters * capacity, dtype=jnp.int32)[:, None]
    ).astype(jnp.bfloat16)
    filled = jnp.sum(placement.astype(jnp.float32), axis=1) > 0.5
    empty_row = jnp.where(
        jnp.arange(features) == 0, jnp.bfloat16(empty_mark), jnp.bfloat16(0)
    ).astype(jnp.bfloat16)
    gathered = jnp.dot(placement, unit_rows, preferred_element_type=jnp.float32).astype(
        jnp.bfloat16
    )
    packed = jnp.where(filled[:, None], gathered, empty_row[None, :])
    arrived = lax.all_to_all(packed, ROUTE, split_axis=0, concat_axis=0, tiled=True)
    slot_mask = (arrived[:, 0].astype(jnp.float32) < 1.5).astype(jnp.float32)
    seeds = seeds16.astype(jnp.float32)
    own = lax.dynamic_slice_in_dim(seeds, first_row, share_rows, 0)
    prototype_lowbits = seeds16
    half_quadratic_length = 0.5 * jnp.sum(seeds * seeds, axis=1)
    for iteration in range(ITERS):
        similarity_logits = (
            jnp.dot(arrived, prototype_lowbits.T, preferred_element_type=jnp.float32)
            - half_quadratic_length[None, :]
        ) / smoothing_scale
        row_max = jnp.max(similarity_logits, axis=1, keepdims=True)
        powers = jnp.exp(similarity_logits - row_max)
        row_sum = jnp.sum(powers, axis=1, keepdims=True)
        weights = (powers / row_sum * slot_mask[:, None]).astype(jnp.bfloat16)
        closing_log_partition = row_max[:, 0] + jnp.log(row_sum[:, 0])
        if iteration + 1 == ITERS:
            energy = (smoothing_scale * closing_log_partition).reshape(-1, members, capacity)
            energy = lax.all_to_all(energy, ("z", "yhi"), split_axis=0, concat_axis=0, tiled=True)
            returned = lax.all_to_all(
                energy, TEAM, split_axis=1, concat_axis=1, tiled=True
            ).reshape(-1)
        weighted = jnp.einsum("rk,rd->kd", weights, arrived, preferred_element_type=jnp.float32)
        masses = jnp.sum(weights.astype(jnp.float32), axis=0)
        combined = jnp.concatenate(
            [
                weighted.reshape(members, share_rows * features),
                jnp.pad(masses.reshape(members, share_rows), ((0, 0), (0, 128 - share_rows))),
            ],
            axis=1,
        )
        width = combined.shape[1]
        by_core = combined.reshape(cores, plane, width)
        mine = lax.dynamic_index_in_dim(by_core, core, 0, keepdims=False)
        theirs = lax.dynamic_index_in_dim(by_core, 1 - core, 0, keepdims=False)
        halves = mine + lax.ppermute(theirs, "core", [(0, 1), (1, 0)])
        if iteration + 1 == ITERS:
            returned, halves = lax.optimization_barrier((returned, halves))
        reduced = jnp.sum(
            lax.all_to_all(halves, PLANE, split_axis=0, concat_axis=0, tiled=True),
            axis=0,
            keepdims=True,
        )
        weighted_own = reduced[0, : share_rows * features].reshape(share_rows, features)
        masses_own = reduced[0, share_rows * features : share_rows * features + share_rows]
        own = (weighted_own + prior_mass * own) / (masses_own + prior_mass)[:, None]
        if iteration + 1 < ITERS:
            half_own = 0.5 * jnp.sum(own * own, axis=1)
            high = lax.reduce_precision(half_own, exponent_bits=8, mantissa_bits=7)
            rest = half_own - high
            middle = lax.reduce_precision(rest, exponent_bits=8, mantissa_bits=7)
            low = rest - middle
            block = jnp.concatenate(
                [
                    own.astype(jnp.bfloat16),
                    jnp.stack([high, middle, low], axis=1).astype(jnp.bfloat16),
                    jnp.zeros((share_rows, 125), jnp.bfloat16),
                ],
                axis=1,
            )
            on_plane = lax.all_to_all(
                jnp.broadcast_to(block[None], (plane,) + block.shape),
                PLANE,
                split_axis=0,
                concat_axis=0,
                tiled=True,
            )
            partner_plane = lax.ppermute(on_plane, "core", [(0, 1), (1, 0)])
            everyone = jnp.concatenate(
                [
                    jnp.where(core == 0, on_plane, partner_plane),
                    jnp.where(core == 0, partner_plane, on_plane),
                ],
                axis=0,
            ).reshape(K, features + 128)
            prototype_lowbits = everyone[:, :features]
            parts = everyone[:, features : features + 3].astype(jnp.float32)
            half_quadratic_length = (parts[:, 0] + parts[:, 1]) + parts[:, 2]
    own_slot = slot_of[None, :] == jnp.arange(clusters * capacity, dtype=jnp.int32)[:, None]
    row_energy = jnp.sum(jnp.where(own_slot, returned[:, None], 0.0), axis=0)
    refined = lax.ppermute(own, ("core", "yhi"), [(0, 0), (1, 2), (2, 1), (3, 3)])
    return (refined, row_energy)


def solution(mesh):
    groups, members = mesh.devices.shape
    fine = Mesh(mesh.devices.reshape(groups // 2, 2, 2, members // 8, 4), ALL)
    in_specs = (P(ALL, None), P(ALL, None), P(("z", "core"), None))
    out_specs = (P(ALL, None), P(ALL))
    return jax.shard_map(shards, mesh=fine, in_specs=in_specs, out_specs=out_specs, check_vma=False)
```

```python
import math

import jax
import jax.numpy as jnp
from jax import lax
from jax.sharding import Mesh
from jax.sharding import PartitionSpec as P

K = 512
ITERS = 2


smoothing_scale = 0.004
prior_mass = 32.0
empty_mark = 2.0


ALL = ("z", "core", "yhi", "ylo", "x")
ROUTE = ("z", "yhi", "core", "ylo", "x")
TEAM = ("core", "ylo", "x")
PLANE = ("ylo", "x")


def shards(embeddings, coarse_ids, centroid_seeds):
    rows_dev, features = embeddings.shape
    cores = lax.axis_size("core")
    plane = lax.axis_size("ylo") * lax.axis_size("x")
    members = cores * plane
    clusters = members * lax.axis_size("z") * lax.axis_size("yhi")
    capacity = 2 * rows_dev // clusters
    share_rows = K // members
    core = lax.axis_index("core")
    yhi = lax.axis_index("yhi")
    spot = lax.axis_index(PLANE)
    first_row = lax.axis_index(TEAM) * share_rows
    partner = lax.ppermute(centroid_seeds, "core", [(0, 1), (1, 0)])
    seeds16 = jnp.where(core == yhi, centroid_seeds, partner)
    widened = embeddings.astype(jnp.float32)
    unit_rows = (
        widened
        * lax.rsqrt(jnp.mean(widened * widened, axis=1, keepdims=True) + 1e-06)
        / math.sqrt(features)
    ).astype(jnp.bfloat16)
    cluster_of = coarse_ids[:, 0]
    onehot = (cluster_of[:, None] == jnp.arange(clusters, dtype=jnp.int32)[None, :]).astype(
        jnp.int32
    )
    row_rank = jnp.sum((jnp.cumsum(onehot, axis=0) - onehot) * onehot, axis=1)
    slot_of = cluster_of * capacity + row_rank
    placement = (
        slot_of[None, :] == jnp.arange(clusters * capacity, dtype=jnp.int32)[:, None]
    ).astype(jnp.bfloat16)
    filled = jnp.sum(placement.astype(jnp.float32), axis=1) > 0.5
    empty_row = jnp.where(
        jnp.arange(features) == 0, jnp.bfloat16(empty_mark), jnp.bfloat16(0)
    ).astype(jnp.bfloat16)
    gathered = jnp.dot(placement, unit_rows, preferred_element_type=jnp.float32).astype(
        jnp.bfloat16
    )
    packed = jnp.where(filled[:, None], gathered, empty_row[None, :])
    arrived = lax.all_to_all(packed, ROUTE, split_axis=0, concat_axis=0, tiled=True)
    slot_mask = (arrived[:, 0].astype(jnp.float32) < 1.5).astype(jnp.float32)
    seeds = seeds16.astype(jnp.float32)
    own = lax.dynamic_slice_in_dim(seeds, first_row, share_rows, 0)
    prototype_lowbits = seeds16
    half_quadratic_length = 0.5 * jnp.sum(seeds * seeds, axis=1)
    for iteration in range(ITERS):
        similarity_logits = (
            jnp.dot(arrived, prototype_lowbits.T, preferred_element_type=jnp.float32)
            - half_quadratic_length[None, :]
        ) / smoothing_scale
        row_max = jnp.max(similarity_logits, axis=1, keepdims=True)
        powers = jnp.exp(similarity_logits - row_max)
        row_sum = jnp.sum(powers, axis=1, keepdims=True)
        weights = (powers / row_sum * slot_mask[:, None]).astype(jnp.bfloat16)
        closing_log_partition = row_max[:, 0] + jnp.log(row_sum[:, 0])
        if iteration + 1 == ITERS:
            returned = lax.all_to_all(
                smoothing_scale * closing_log_partition, ROUTE, split_axis=0, concat_axis=0,
                tiled=True,
            )
        weighted = jnp.einsum("rk,rd->kd", weights, arrived, preferred_element_type=jnp.float32)
        masses = jnp.sum(weights.astype(jnp.float32), axis=0)
        combined = jnp.concatenate(
            [
                weighted.reshape(members, share_rows * features),
                jnp.pad(masses.reshape(members, share_rows), ((0, 0), (0, 128 - share_rows))),
            ],
            axis=1,
        )
        width = combined.shape[1]
        by_core = combined.reshape(cores, plane, width)
        mine = lax.dynamic_index_in_dim(by_core, core, 0, keepdims=False)
        theirs = lax.dynamic_index_in_dim(by_core, 1 - core, 0, keepdims=False)
        halves = mine + lax.ppermute(theirs, "core", [(0, 1), (1, 0)])
        if iteration + 1 == ITERS:
            returned, halves = lax.optimization_barrier((returned, halves))
        reduced = lax.dynamic_index_in_dim(halves, spot, 0, keepdims=True)
        for shift in range(1, plane):
            outgoing = lax.dynamic_index_in_dim(halves, (spot + shift) % plane, 0, keepdims=True)
            reduced = reduced + lax.ppermute(
                outgoing, PLANE, [(i, (i + shift) % plane) for i in range(plane)]
            )
        weighted_own = reduced[0, : share_rows * features].reshape(share_rows, features)
        masses_own = reduced[0, share_rows * features : share_rows * features + share_rows]
        own = (weighted_own + prior_mass * own) / (masses_own + prior_mass)[:, None]
        if iteration + 1 < ITERS:
            half_own = 0.5 * jnp.sum(own * own, axis=1)
            high = lax.reduce_precision(half_own, exponent_bits=8, mantissa_bits=7)
            rest = half_own - high
            middle = lax.reduce_precision(rest, exponent_bits=8, mantissa_bits=7)
            low = rest - middle
            block = jnp.concatenate(
                [
                    own.astype(jnp.bfloat16),
                    jnp.stack([high, middle, low], axis=1).astype(jnp.bfloat16),
                    jnp.zeros((share_rows, 125), jnp.bfloat16),
                ],
                axis=1,
            )
            by_shift = jnp.stack(
                [block]
                + [
                    lax.ppermute(block, PLANE, [(i, (i + shift) % plane) for i in range(plane)])
                    for shift in range(1, plane)
                ]
            )
            on_plane = jnp.take(by_shift, (spot - jnp.arange(plane)) % plane, axis=0)
            partner_plane = lax.ppermute(on_plane, "core", [(0, 1), (1, 0)])
            everyone = jnp.concatenate(
                [
                    jnp.where(core == 0, on_plane, partner_plane),
                    jnp.where(core == 0, partner_plane, on_plane),
                ],
                axis=0,
            ).reshape(K, features + 128)
            prototype_lowbits = everyone[:, :features]
            parts = everyone[:, features : features + 3].astype(jnp.float32)
            half_quadratic_length = (parts[:, 0] + parts[:, 1]) + parts[:, 2]
    own_slot = slot_of[None, :] == jnp.arange(clusters * capacity, dtype=jnp.int32)[:, None]
    row_energy = jnp.sum(jnp.where(own_slot, returned[:, None], 0.0), axis=0)
    refined = lax.ppermute(own, ("core", "yhi"), [(0, 0), (1, 2), (2, 1), (3, 3)])
    return (refined, row_energy)


def solution(mesh):
    groups, members = mesh.devices.shape
    fine = Mesh(mesh.devices.reshape(groups // 2, 2, 2, members // 8, 4), ALL)
    in_specs = (P(ALL, None), P(ALL, None), P(("z", "core"), None))
    out_specs = (P(ALL, None), P(ALL))
    return jax.shard_map(shards, mesh=fine, in_specs=in_specs, out_specs=out_specs, check_vma=False)
```

```python
import math

import jax
import jax.numpy as jnp
from jax import lax
from jax.sharding import Mesh
from jax.sharding import PartitionSpec as P


K = 512
ITERS = 2


smoothing_scale = 0.004
prior_mass = 32.0
empty_mark = 2.0


ALL = ("z", "core", "yhi", "ylo", "x")
ROUTE = ("z", "yhi", "core", "ylo", "x")
TEAM = ("core", "ylo", "x")
PLANE = ("ylo", "x")


def steps(embeddings, coarse_ids, centroid_seeds):
    rows_dev, features = embeddings.shape
    cores = lax.axis_size("core")
    plane = lax.axis_size("ylo") * lax.axis_size("x")
    members = cores * plane
    clusters = members * lax.axis_size("z") * lax.axis_size("yhi")
    capacity = 2 * rows_dev // clusters
    share_rows = K // members
    core = lax.axis_index("core")
    yhi = lax.axis_index("yhi")
    spot = lax.axis_index(PLANE)
    first_row = lax.axis_index(TEAM) * share_rows
    partner = lax.ppermute(centroid_seeds, "core", [(0, 1), (1, 0)])
    seeds16 = jnp.where(core == yhi, centroid_seeds, partner)
    widened = embeddings.astype(jnp.float32)
    unit_rows = (
        widened
        * lax.rsqrt(jnp.mean(widened * widened, axis=1, keepdims=True) + 1e-06)
        / math.sqrt(features)
    ).astype(jnp.bfloat16)
    cluster_of = coarse_ids[:, 0]
    onehot = (cluster_of[:, None] == jnp.arange(clusters, dtype=jnp.int32)[None, :]).astype(
        jnp.int32
    )
    row_rank = jnp.sum((jnp.cumsum(onehot, axis=0) - onehot) * onehot, axis=1)
    slot_of = cluster_of * capacity + row_rank
    placement = (
        slot_of[None, :] == jnp.arange(clusters * capacity, dtype=jnp.int32)[:, None]
    ).astype(jnp.bfloat16)
    filled = jnp.sum(placement.astype(jnp.float32), axis=1) > 0.5
    empty_row = jnp.where(
        jnp.arange(features) == 0, jnp.bfloat16(empty_mark), jnp.bfloat16(0)
    ).astype(jnp.bfloat16)
    gathered = jnp.dot(placement, unit_rows, preferred_element_type=jnp.float32).astype(
        jnp.bfloat16
    )
    packed = jnp.where(filled[:, None], gathered, empty_row[None, :])
    arrived = lax.all_to_all(packed, ROUTE, split_axis=0, concat_axis=0, tiled=True)
    slot_mask = (arrived[:, 0].astype(jnp.float32) < 1.5).astype(jnp.float32)
    seeds = seeds16.astype(jnp.float32)
    own = lax.dynamic_slice_in_dim(seeds, first_row, share_rows, 0)
    prototype_lowbits = seeds16
    half_quadratic_length = 0.5 * jnp.sum(seeds * seeds, axis=1)
    for iteration in range(ITERS):
        similarity_logits = (
            jnp.dot(arrived, prototype_lowbits.T, preferred_element_type=jnp.float32)
            - half_quadratic_length[None, :]
        ) / smoothing_scale
        row_max = jnp.max(similarity_logits, axis=1, keepdims=True)
        powers = jnp.exp(similarity_logits - row_max)
        row_sum = jnp.sum(powers, axis=1, keepdims=True)
        weights = (powers / row_sum * slot_mask[:, None]).astype(jnp.bfloat16)
        closing_log_partition = row_max[:, 0] + jnp.log(row_sum[:, 0])
        if iteration + 1 == ITERS:
            returned = lax.all_to_all(
                smoothing_scale * closing_log_partition, ROUTE, split_axis=0, concat_axis=0,
                tiled=True,
            )
        weighted = jnp.einsum("rk,rd->kd", weights, arrived, preferred_element_type=jnp.float32)
        masses = jnp.sum(weights.astype(jnp.float32), axis=0)
        combined = jnp.concatenate(
            [
                weighted.reshape(members, share_rows * features),
                jnp.pad(masses.reshape(members, share_rows), ((0, 0), (0, 128 - share_rows))),
            ],
            axis=1,
        )
        width = combined.shape[1]
        by_core = combined.reshape(cores, plane, width)
        mine = lax.dynamic_index_in_dim(by_core, core, 0, keepdims=False)
        theirs = lax.dynamic_index_in_dim(by_core, 1 - core, 0, keepdims=False)
        halves = mine + lax.ppermute(theirs, "core", [(0, 1), (1, 0)])
        reduced = lax.dynamic_index_in_dim(halves, spot, 0, keepdims=True)
        for shift in range(1, plane):
            outgoing = lax.dynamic_index_in_dim(halves, (spot + shift) % plane, 0, keepdims=True)
            incoming = lax.ppermute(
                outgoing, PLANE, [(i, (i + shift) % plane) for i in range(plane)]
            )
            reduced = reduced + incoming
        weighted_own = reduced[0, : share_rows * features].reshape(share_rows, features)
        masses_own = reduced[0, share_rows * features : share_rows * features + share_rows]
        own = (weighted_own + prior_mass * own) / (masses_own + prior_mass)[:, None]
        if iteration + 1 < ITERS:
            half_own = 0.5 * jnp.sum(own * own, axis=1)
            high = lax.reduce_precision(half_own, exponent_bits=8, mantissa_bits=7)
            rest = half_own - high
            middle = lax.reduce_precision(rest, exponent_bits=8, mantissa_bits=7)
            low = rest - middle
            block = jnp.concatenate(
                [
                    own.astype(jnp.bfloat16),
                    jnp.stack([high, middle, low], axis=1).astype(jnp.bfloat16),
                    jnp.zeros((share_rows, 125), jnp.bfloat16),
                ],
                axis=1,
            )
            by_shift = jnp.stack(
                [block]
                + [
                    lax.ppermute(block, PLANE, [(i, (i + shift) % plane) for i in range(plane)])
                    for shift in range(1, plane)
                ]
            )
            on_plane = jnp.take(by_shift, (spot - jnp.arange(plane)) % plane, axis=0)
            partner_plane = lax.ppermute(on_plane, "core", [(0, 1), (1, 0)])
            everyone = jnp.concatenate(
                [
                    jnp.where(core == 0, on_plane, partner_plane),
                    jnp.where(core == 0, partner_plane, on_plane),
                ],
                axis=0,
            ).reshape(K, features + 128)
            prototype_lowbits = everyone[:, :features]
            parts = everyone[:, features : features + 3].astype(jnp.float32)
            half_quadratic_length = (parts[:, 0] + parts[:, 1]) + parts[:, 2]
    own_slot = slot_of[None, :] == jnp.arange(clusters * capacity, dtype=jnp.int32)[:, None]
    row_energy = jnp.sum(jnp.where(own_slot, returned[:, None], 0.0), axis=0)
    refined = lax.ppermute(own, ("core", "yhi"), [(0, 0), (1, 2), (2, 1), (3, 3)])
    return (refined, row_energy)


def solution(mesh):
    groups, members = mesh.devices.shape
    fine = Mesh(mesh.devices.reshape(groups // 2, 2, 2, members // 8, 4), ALL)
    in_specs = (P(ALL, None), P(ALL, None), P(("z", "core"), None))
    out_specs = (P(ALL, None), P(ALL))
    return jax.shard_map(steps, mesh=fine, in_specs=in_specs, out_specs=out_specs, check_vma=False)
```

```python
import math

import jax
import jax.numpy as jnp
from jax import lax
from jax.sharding import Mesh
from jax.sharding import PartitionSpec as P


K = 512
ITERS = 2


smoothing_scale = 0.004
prior_mass = 32.0
empty_mark = 2.0


ALL = ("z", "core", "yhi", "ylo", "x")
ROUTE = ("z", "yhi", "core", "ylo", "x")
TEAM = ("core", "ylo", "x")
PLANE = ("ylo", "x")


def steps(embeddings, coarse_ids, centroid_seeds):
    rows_dev, features = embeddings.shape
    cores = lax.axis_size("core")
    plane = lax.axis_size("ylo") * lax.axis_size("x")
    members = cores * plane
    clusters = members * lax.axis_size("z") * lax.axis_size("yhi")
    capacity = 2 * rows_dev // clusters
    share_rows = K // members
    core = lax.axis_index("core")
    yhi = lax.axis_index("yhi")
    spot = lax.axis_index(PLANE)
    first_row = lax.axis_index(TEAM) * share_rows
    partner = lax.ppermute(centroid_seeds, "core", [(0, 1), (1, 0)])
    seeds16 = jnp.where(core == yhi, centroid_seeds, partner)
    widened = embeddings.astype(jnp.float32)
    unit_rows = (
        widened
        * lax.rsqrt(jnp.mean(widened * widened, axis=1, keepdims=True) + 1e-06)
        / math.sqrt(features)
    ).astype(jnp.bfloat16)
    cluster_of = coarse_ids[:, 0]
    onehot = (cluster_of[:, None] == jnp.arange(clusters, dtype=jnp.int32)[None, :]).astype(
        jnp.int32
    )
    row_rank = jnp.sum((jnp.cumsum(onehot, axis=0) - onehot) * onehot, axis=1)
    slot_of = cluster_of * capacity + row_rank
    placement = (
        slot_of[None, :] == jnp.arange(clusters * capacity, dtype=jnp.int32)[:, None]
    ).astype(jnp.bfloat16)
    filled = jnp.sum(placement.astype(jnp.float32), axis=1) > 0.5
    empty_row = jnp.where(
        jnp.arange(features) == 0, jnp.bfloat16(empty_mark), jnp.bfloat16(0)
    ).astype(jnp.bfloat16)
    gathered = jnp.dot(placement, unit_rows, preferred_element_type=jnp.float32).astype(
        jnp.bfloat16
    )
    packed = jnp.where(filled[:, None], gathered, empty_row[None, :])
    arrived = lax.all_to_all(packed, ROUTE, split_axis=0, concat_axis=0, tiled=True)
    slot_mask = (arrived[:, 0].astype(jnp.float32) < 1.5).astype(jnp.float32)
    seeds = seeds16.astype(jnp.float32)
    own = lax.dynamic_slice_in_dim(seeds, first_row, share_rows, 0)
    prototype_lowbits = seeds16
    half_quadratic_length = 0.5 * jnp.sum(seeds * seeds, axis=1)
    for iteration in range(ITERS):
        similarity_logits = (
            jnp.dot(arrived, prototype_lowbits.T, preferred_element_type=jnp.float32)
            - half_quadratic_length[None, :]
        ) / smoothing_scale
        row_max = jnp.max(similarity_logits, axis=1, keepdims=True)
        powers = jnp.exp(similarity_logits - row_max)
        row_sum = jnp.sum(powers, axis=1, keepdims=True)
        weights = (powers / row_sum * slot_mask[:, None]).astype(jnp.bfloat16)
        closing_log_partition = row_max[:, 0] + jnp.log(row_sum[:, 0])
        if iteration + 1 == ITERS:
            returned = lax.all_to_all(
                smoothing_scale * closing_log_partition, ROUTE, split_axis=0, concat_axis=0,
                tiled=True,
            )
        half_rows = K // cores

        def block_sums(side):
            picked = lax.dynamic_slice_in_dim(weights, side * half_rows, half_rows, 1)
            weighted = jnp.einsum(
                "rk,rd->kd", picked, arrived, preferred_element_type=jnp.float32
            )
            masses = jnp.sum(picked.astype(jnp.float32), axis=0)
            return jnp.concatenate(
                [
                    weighted.reshape(plane, share_rows * features),
                    jnp.pad(masses.reshape(plane, share_rows), ((0, 0), (0, 128 - share_rows))),
                ],
                axis=1,
            )

        incoming = lax.ppermute(block_sums(1 - core), "core", [(0, 1), (1, 0)])
        halves = block_sums(core) + incoming
        reduced = lax.dynamic_index_in_dim(halves, spot, 0, keepdims=True)
        for shift in range(1, plane):
            outgoing = lax.dynamic_index_in_dim(halves, (spot + shift) % plane, 0, keepdims=True)
            incoming = lax.ppermute(
                outgoing, PLANE, [(i, (i + shift) % plane) for i in range(plane)]
            )
            reduced = reduced + incoming
        weighted_own = reduced[0, : share_rows * features].reshape(share_rows, features)
        masses_own = reduced[0, share_rows * features : share_rows * features + share_rows]
        own = (weighted_own + prior_mass * own) / (masses_own + prior_mass)[:, None]
        if iteration + 1 < ITERS:
            half_own = 0.5 * jnp.sum(own * own, axis=1)
            high = lax.reduce_precision(half_own, exponent_bits=8, mantissa_bits=7)
            rest = half_own - high
            middle = lax.reduce_precision(rest, exponent_bits=8, mantissa_bits=7)
            low = rest - middle
            block = jnp.concatenate(
                [
                    own.astype(jnp.bfloat16),
                    jnp.stack([high, middle, low], axis=1).astype(jnp.bfloat16),
                    jnp.zeros((share_rows, 125), jnp.bfloat16),
                ],
                axis=1,
            )
            by_shift = jnp.stack(
                [block]
                + [
                    lax.ppermute(block, PLANE, [(i, (i + shift) % plane) for i in range(plane)])
                    for shift in range(1, plane)
                ]
            )
            on_plane = jnp.take(by_shift, (spot - jnp.arange(plane)) % plane, axis=0)
            partner_plane = lax.ppermute(on_plane, "core", [(0, 1), (1, 0)])
            everyone = jnp.concatenate(
                [
                    jnp.where(core == 0, on_plane, partner_plane),
                    jnp.where(core == 0, partner_plane, on_plane),
                ],
                axis=0,
            ).reshape(K, features + 128)
            prototype_lowbits = everyone[:, :features]
            parts = everyone[:, features : features + 3].astype(jnp.float32)
            half_quadratic_length = (parts[:, 0] + parts[:, 1]) + parts[:, 2]
    own_slot = slot_of[None, :] == jnp.arange(clusters * capacity, dtype=jnp.int32)[:, None]
    row_energy = jnp.sum(jnp.where(own_slot, returned[:, None], 0.0), axis=0)
    refined = lax.ppermute(own, ("core", "yhi"), [(0, 0), (1, 2), (2, 1), (3, 3)])
    return (refined, row_energy)


def solution(mesh):
    groups, members = mesh.devices.shape
    fine = Mesh(mesh.devices.reshape(groups // 2, 2, 2, members // 8, 4), ALL)
    in_specs = (P(ALL, None), P(ALL, None), P(("z", "core"), None))
    out_specs = (P(ALL, None), P(ALL))
    return jax.shard_map(steps, mesh=fine, in_specs=in_specs, out_specs=out_specs, check_vma=False)
```

```python
import math

import jax
import jax.numpy as jnp
from jax import lax
from jax.sharding import Mesh
from jax.sharding import PartitionSpec as P


K = 512
ITERS = 2


smoothing_scale = 0.004
prior_mass = 32.0
empty_mark = 2.0


ALL = ("z", "core", "yhi", "ylo", "x")
ROUTE = ("z", "yhi", "core", "ylo", "x")
TEAM = ("core", "ylo", "x")
PLANE = ("ylo", "x")


def steps(embeddings, coarse_ids, centroid_seeds):
    rows_dev, features = embeddings.shape
    cores = lax.axis_size("core")
    plane = lax.axis_size("ylo") * lax.axis_size("x")
    members = cores * plane
    clusters = members * lax.axis_size("z") * lax.axis_size("yhi")
    capacity = 2 * rows_dev // clusters
    share_rows = K // members
    core = lax.axis_index("core")
    yhi = lax.axis_index("yhi")
    spot = lax.axis_index(PLANE)
    first_row = lax.axis_index(TEAM) * share_rows
    partner = lax.ppermute(centroid_seeds, "core", [(0, 1), (1, 0)])
    seeds16 = jnp.where(core == yhi, centroid_seeds, partner)
    widened = embeddings.astype(jnp.float32)
    unit_rows = (
        widened
        * lax.rsqrt(jnp.mean(widened * widened, axis=1, keepdims=True) + 1e-06)
        / math.sqrt(features)
    ).astype(jnp.bfloat16)
    cluster_of = coarse_ids[:, 0]
    onehot = (cluster_of[:, None] == jnp.arange(clusters, dtype=jnp.int32)[None, :]).astype(
        jnp.int32
    )
    row_rank = jnp.sum((jnp.cumsum(onehot, axis=0) - onehot) * onehot, axis=1)
    slot_of = cluster_of * capacity + row_rank
    placement = (
        slot_of[None, :] == jnp.arange(clusters * capacity, dtype=jnp.int32)[:, None]
    ).astype(jnp.bfloat16)
    filled = jnp.sum(placement.astype(jnp.float32), axis=1) > 0.5
    empty_row = jnp.where(
        jnp.arange(features) == 0, jnp.bfloat16(empty_mark), jnp.bfloat16(0)
    ).astype(jnp.bfloat16)
    gathered = jnp.dot(placement, unit_rows, preferred_element_type=jnp.float32).astype(
        jnp.bfloat16
    )
    packed = jnp.where(filled[:, None], gathered, empty_row[None, :])
    arrived = lax.all_to_all(packed, ROUTE, split_axis=0, concat_axis=0, tiled=True)
    slot_mask = (arrived[:, 0].astype(jnp.float32) < 1.5).astype(jnp.float32)
    seeds = seeds16.astype(jnp.float32)
    own = lax.dynamic_slice_in_dim(seeds, first_row, share_rows, 0)
    prototype_lowbits = seeds16
    half_quadratic_length = 0.5 * jnp.sum(seeds * seeds, axis=1)
    for iteration in range(ITERS):
        similarity_logits = (
            jnp.dot(arrived, prototype_lowbits.T, preferred_element_type=jnp.float32)
            - half_quadratic_length[None, :]
        ) / smoothing_scale
        row_max = jnp.max(similarity_logits, axis=1, keepdims=True)
        powers = jnp.exp(similarity_logits - row_max)
        row_sum = jnp.sum(powers, axis=1, keepdims=True)
        weights = (powers / row_sum * slot_mask[:, None]).astype(jnp.bfloat16)
        closing_log_partition = row_max[:, 0] + jnp.log(row_sum[:, 0])
        if iteration + 1 == ITERS:
            returned = lax.all_to_all(
                smoothing_scale * closing_log_partition, ROUTE, split_axis=0, concat_axis=0,
                tiled=True,
            )
        weighted = jnp.einsum("rk,rd->kd", weights, arrived, preferred_element_type=jnp.float32)
        masses = jnp.sum(weights.astype(jnp.float32), axis=0)
        combined = jnp.concatenate(
            [
                weighted.reshape(members, share_rows * features),
                jnp.pad(masses.reshape(members, share_rows), ((0, 0), (0, 128 - share_rows))),
            ],
            axis=1,
        )
        width = combined.shape[1]
        by_core = combined.reshape(cores, plane, width)
        mine = lax.dynamic_index_in_dim(by_core, core, 0, keepdims=False)
        theirs = lax.dynamic_index_in_dim(by_core, 1 - core, 0, keepdims=False)
        halves = mine + lax.ppermute(theirs, "core", [(0, 1), (1, 0)])
        reduced = lax.dynamic_index_in_dim(halves, spot, 0, keepdims=True)
        for shift in range(1, plane):
            outgoing = lax.dynamic_index_in_dim(halves, (spot + shift) % plane, 0, keepdims=True)
            incoming = lax.ppermute(
                outgoing, PLANE, [(i, (i + shift) % plane) for i in range(plane)]
            )
            reduced = reduced + incoming
        weighted_own = reduced[0, : share_rows * features].reshape(share_rows, features)
        masses_own = reduced[0, share_rows * features : share_rows * features + share_rows]
        own = (weighted_own + prior_mass * own) / (masses_own + prior_mass)[:, None]
        if iteration + 1 < ITERS:
            half_own = 0.5 * jnp.sum(own * own, axis=1)
            high = lax.reduce_precision(half_own, exponent_bits=8, mantissa_bits=7)
            rest = half_own - high
            middle = lax.reduce_precision(rest, exponent_bits=8, mantissa_bits=7)
            low = rest - middle
            block = jnp.concatenate(
                [
                    own.astype(jnp.bfloat16),
                    jnp.stack([high, middle, low], axis=1).astype(jnp.bfloat16),
                    jnp.zeros((share_rows, 125), jnp.bfloat16),
                ],
                axis=1,
            )
            on_plane = lax.all_to_all(
                jnp.broadcast_to(block[None], (plane,) + block.shape),
                PLANE,
                split_axis=0,
                concat_axis=0,
                tiled=True,
            )
            partner_plane = lax.ppermute(on_plane, "core", [(0, 1), (1, 0)])
            everyone = jnp.concatenate(
                [
                    jnp.where(core == 0, on_plane, partner_plane),
                    jnp.where(core == 0, partner_plane, on_plane),
                ],
                axis=0,
            ).reshape(K, features + 128)
            prototype_lowbits = everyone[:, :features]
            parts = everyone[:, features : features + 3].astype(jnp.float32)
            half_quadratic_length = (parts[:, 0] + parts[:, 1]) + parts[:, 2]
    own_slot = slot_of[None, :] == jnp.arange(clusters * capacity, dtype=jnp.int32)[:, None]
    row_energy = jnp.sum(jnp.where(own_slot, returned[:, None], 0.0), axis=0)
    refined = lax.ppermute(own, ("core", "yhi"), [(0, 0), (1, 2), (2, 1), (3, 3)])
    return (refined, row_energy)


def solution(mesh):
    groups, members = mesh.devices.shape
    fine = Mesh(mesh.devices.reshape(groups // 2, 2, 2, members // 8, 4), ALL)
    in_specs = (P(ALL, None), P(ALL, None), P(("z", "core"), None))
    out_specs = (P(ALL, None), P(ALL))
    return jax.shard_map(steps, mesh=fine, in_specs=in_specs, out_specs=out_specs, check_vma=False)
```

```python
import math

import jax
import jax.numpy as jnp
from jax import lax
from jax.sharding import Mesh
from jax.sharding import PartitionSpec as P


K = 512
ITERS = 2


smoothing_scale = 0.004
prior_mass = 32.0
empty_mark = 2.0


ALL = ("z", "core", "yhi", "ylo", "x")
ROUTE = ("z", "yhi", "core", "ylo", "x")
TEAM = ("core", "ylo", "x")
PLANE = ("ylo", "x")


def steps(embeddings, coarse_ids, centroid_seeds):
    rows_dev, features = embeddings.shape
    cores = lax.axis_size("core")
    plane = lax.axis_size("ylo") * lax.axis_size("x")
    members = cores * plane
    clusters = members * lax.axis_size("z") * lax.axis_size("yhi")
    capacity = 2 * rows_dev // clusters
    share_rows = K // members
    core = lax.axis_index("core")
    yhi = lax.axis_index("yhi")
    first_row = lax.axis_index(TEAM) * share_rows
    partner = lax.ppermute(centroid_seeds, "core", [(0, 1), (1, 0)])
    seeds16 = jnp.where(core == yhi, centroid_seeds, partner)
    widened = embeddings.astype(jnp.float32)
    unit_rows = (
        widened
        * lax.rsqrt(jnp.mean(widened * widened, axis=1, keepdims=True) + 1e-06)
        / math.sqrt(features)
    ).astype(jnp.bfloat16)
    cluster_of = coarse_ids[:, 0]
    onehot = (cluster_of[:, None] == jnp.arange(clusters, dtype=jnp.int32)[None, :]).astype(
        jnp.int32
    )
    row_rank = jnp.sum((jnp.cumsum(onehot, axis=0) - onehot) * onehot, axis=1)
    slot_of = cluster_of * capacity + row_rank
    placement = (
        slot_of[None, :] == jnp.arange(clusters * capacity, dtype=jnp.int32)[:, None]
    ).astype(jnp.bfloat16)
    filled = jnp.sum(placement.astype(jnp.float32), axis=1) > 0.5
    empty_row = jnp.where(
        jnp.arange(features) == 0, jnp.bfloat16(empty_mark), jnp.bfloat16(0)
    ).astype(jnp.bfloat16)
    gathered = jnp.dot(placement, unit_rows, preferred_element_type=jnp.float32).astype(
        jnp.bfloat16
    )
    packed = jnp.where(filled[:, None], gathered, empty_row[None, :])
    arrived = lax.all_to_all(packed, ROUTE, split_axis=0, concat_axis=0, tiled=True)
    slot_mask = (arrived[:, 0].astype(jnp.float32) < 1.5).astype(jnp.float32)
    seeds = seeds16.astype(jnp.float32)
    own = lax.dynamic_slice_in_dim(seeds, first_row, share_rows, 0)
    prototype_lowbits = seeds16
    half_quadratic_length = 0.5 * jnp.sum(seeds * seeds, axis=1)
    for iteration in range(ITERS):
        similarity_logits = (
            jnp.dot(arrived, prototype_lowbits.T, preferred_element_type=jnp.float32)
            - half_quadratic_length[None, :]
        ) / smoothing_scale
        row_max = jnp.max(similarity_logits, axis=1, keepdims=True)
        powers = jnp.exp(similarity_logits - row_max)
        row_sum = jnp.sum(powers, axis=1, keepdims=True)
        weights = (powers / row_sum * slot_mask[:, None]).astype(jnp.bfloat16)
        closing_log_partition = row_max[:, 0] + jnp.log(row_sum[:, 0])
        if iteration + 1 == ITERS:
            returned = lax.all_to_all(
                smoothing_scale * closing_log_partition, ROUTE, split_axis=0, concat_axis=0,
                tiled=True,
            )
        weighted = jnp.einsum("rk,rd->kd", weights, arrived, preferred_element_type=jnp.float32)
        masses = jnp.sum(weights.astype(jnp.float32), axis=0)
        combined = jnp.concatenate(
            [
                weighted.reshape(members, share_rows * features),
                jnp.pad(masses.reshape(members, share_rows), ((0, 0), (0, 128 - share_rows))),
            ],
            axis=1,
        )
        width = combined.shape[1]
        by_core = combined.reshape(cores, plane, width)
        mine = lax.dynamic_index_in_dim(by_core, core, 0, keepdims=False)
        theirs = lax.dynamic_index_in_dim(by_core, 1 - core, 0, keepdims=False)
        halves = mine + lax.ppermute(theirs, "core", [(0, 1), (1, 0)])
        lanes = lax.axis_size("x")
        ylo = lax.axis_index("ylo")
        column = lax.axis_index("x")
        by_row = halves.reshape(-1, lanes, halves.shape[1])
        mine_row = lax.dynamic_index_in_dim(by_row, ylo, 0, keepdims=False)
        other_row = lax.dynamic_index_in_dim(by_row, 1 - ylo, 0, keepdims=False)
        other_row = lax.ppermute(other_row, "ylo", [(0, 1), (1, 0)])
        row_sums = mine_row + other_row
        reduced = lax.dynamic_index_in_dim(row_sums, column, 0, keepdims=True)
        for shift in range(1, lanes):
            outgoing = lax.dynamic_index_in_dim(row_sums, (column + shift) % lanes, 0, keepdims=True)
            incoming = lax.ppermute(outgoing, "x", [(i, (i + shift) % lanes) for i in range(lanes)])
            reduced = reduced + incoming
        weighted_own = reduced[0, : share_rows * features].reshape(share_rows, features)
        masses_own = reduced[0, share_rows * features : share_rows * features + share_rows]
        own = (weighted_own + prior_mass * own) / (masses_own + prior_mass)[:, None]
        if iteration + 1 < ITERS:
            half_own = 0.5 * jnp.sum(own * own, axis=1)
            high = lax.reduce_precision(half_own, exponent_bits=8, mantissa_bits=7)
            rest = half_own - high
            middle = lax.reduce_precision(rest, exponent_bits=8, mantissa_bits=7)
            low = rest - middle
            block = jnp.concatenate(
                [
                    own.astype(jnp.bfloat16),
                    jnp.stack([high, middle, low], axis=1).astype(jnp.bfloat16),
                    jnp.zeros((share_rows, 125), jnp.bfloat16),
                ],
                axis=1,
            )
            on_plane = lax.all_to_all(
                jnp.broadcast_to(block[None], (plane,) + block.shape),
                PLANE,
                split_axis=0,
                concat_axis=0,
                tiled=True,
            )
            partner_plane = lax.ppermute(on_plane, "core", [(0, 1), (1, 0)])
            everyone = jnp.concatenate(
                [
                    jnp.where(core == 0, on_plane, partner_plane),
                    jnp.where(core == 0, partner_plane, on_plane),
                ],
                axis=0,
            ).reshape(K, features + 128)
            prototype_lowbits = everyone[:, :features]
            parts = everyone[:, features : features + 3].astype(jnp.float32)
            half_quadratic_length = (parts[:, 0] + parts[:, 1]) + parts[:, 2]
    own_slot = slot_of[None, :] == jnp.arange(clusters * capacity, dtype=jnp.int32)[:, None]
    row_energy = jnp.sum(jnp.where(own_slot, returned[:, None], 0.0), axis=0)
    refined = lax.ppermute(own, ("core", "yhi"), [(0, 0), (1, 2), (2, 1), (3, 3)])
    return (refined, row_energy)


def solution(mesh):
    groups, members = mesh.devices.shape
    fine = Mesh(mesh.devices.reshape(groups // 2, 2, 2, members // 8, 4), ALL)
    in_specs = (P(ALL, None), P(ALL, None), P(("z", "core"), None))
    out_specs = (P(ALL, None), P(ALL))
    return jax.shard_map(steps, mesh=fine, in_specs=in_specs, out_specs=out_specs, check_vma=False)
```

```python
import math

import jax
import jax.numpy as jnp
from jax import lax
from jax.sharding import Mesh
from jax.sharding import PartitionSpec as P


K = 512
ITERS = 2


smoothing_scale = 0.004
prior_mass = 32.0
empty_mark = 2.0


ALL = ("z", "core", "yhi", "ylo", "x")
ROUTE = ("z", "yhi", "core", "ylo", "x")
TEAM = ("core", "ylo", "x")
PLANE = ("ylo", "x")


def steps(embeddings, coarse_ids, centroid_seeds):
    rows_dev, features = embeddings.shape
    cores = lax.axis_size("core")
    plane = lax.axis_size("ylo") * lax.axis_size("x")
    members = cores * plane
    clusters = members * lax.axis_size("z") * lax.axis_size("yhi")
    capacity = 2 * rows_dev // clusters
    share_rows = K // members
    core = lax.axis_index("core")
    yhi = lax.axis_index("yhi")
    spot = lax.axis_index(PLANE)
    first_row = lax.axis_index(TEAM) * share_rows
    partner = lax.ppermute(centroid_seeds, "core", [(0, 1), (1, 0)])
    seeds16 = jnp.where(core == yhi, centroid_seeds, partner)
    widened = embeddings.astype(jnp.float32)
    unit_rows = (
        widened
        * lax.rsqrt(jnp.mean(widened * widened, axis=1, keepdims=True) + 1e-06)
        / math.sqrt(features)
    ).astype(jnp.bfloat16)
    cluster_of = coarse_ids[:, 0]
    onehot = (cluster_of[:, None] == jnp.arange(clusters, dtype=jnp.int32)[None, :]).astype(
        jnp.int32
    )
    row_rank = jnp.sum((jnp.cumsum(onehot, axis=0) - onehot) * onehot, axis=1)
    slot_of = cluster_of * capacity + row_rank
    placement = (
        slot_of[None, :] == jnp.arange(clusters * capacity, dtype=jnp.int32)[:, None]
    ).astype(jnp.bfloat16)
    filled = jnp.sum(placement.astype(jnp.float32), axis=1) > 0.5
    empty_row = jnp.where(
        jnp.arange(features) == 0, jnp.bfloat16(empty_mark), jnp.bfloat16(0)
    ).astype(jnp.bfloat16)
    gathered = jnp.dot(placement, unit_rows, preferred_element_type=jnp.float32).astype(
        jnp.bfloat16
    )
    packed = jnp.where(filled[:, None], gathered, empty_row[None, :])
    arrived = lax.all_to_all(packed, ROUTE, split_axis=0, concat_axis=0, tiled=True)
    slot_mask = (arrived[:, 0].astype(jnp.float32) < 1.5).astype(jnp.float32)
    widened_rows = jnp.concatenate(
        [
            arrived,
            jnp.ones((arrived.shape[0], 1), jnp.bfloat16),
            jnp.zeros((arrived.shape[0], 127), jnp.bfloat16),
        ],
        axis=1,
    )
    seeds = seeds16.astype(jnp.float32)
    own = lax.dynamic_slice_in_dim(seeds, first_row, share_rows, 0)
    prototype_lowbits = seeds16
    half_quadratic_length = 0.5 * jnp.sum(seeds * seeds, axis=1)
    for iteration in range(ITERS):
        similarity_logits = (
            jnp.dot(arrived, prototype_lowbits.T, preferred_element_type=jnp.float32)
            - half_quadratic_length[None, :]
        ) / smoothing_scale
        row_max = jnp.max(similarity_logits, axis=1, keepdims=True)
        powers = jnp.exp(similarity_logits - row_max)
        row_sum = jnp.sum(powers, axis=1, keepdims=True)
        weights = (powers / row_sum * slot_mask[:, None]).astype(jnp.bfloat16)
        closing_log_partition = row_max[:, 0] + jnp.log(row_sum[:, 0])
        if iteration + 1 == ITERS:
            returned = lax.all_to_all(
                smoothing_scale * closing_log_partition, ROUTE, split_axis=0, concat_axis=0,
                tiled=True,
            )
        weighted = jnp.einsum(
            "rk,rd->kd", weights, widened_rows, preferred_element_type=jnp.float32
        )
        by_core = weighted.reshape(cores, plane, share_rows, features + 128)
        mine = lax.dynamic_index_in_dim(by_core, core, 0, keepdims=False)
        theirs = lax.dynamic_index_in_dim(by_core, 1 - core, 0, keepdims=False)
        halves = mine + lax.ppermute(theirs, "core", [(0, 1), (1, 0)])
        reduced = lax.dynamic_index_in_dim(halves, spot, 0, keepdims=True)
        for shift in range(1, plane):
            outgoing = lax.dynamic_index_in_dim(halves, (spot + shift) % plane, 0, keepdims=True)
            incoming = lax.ppermute(
                outgoing, PLANE, [(i, (i + shift) % plane) for i in range(plane)]
            )
            reduced = reduced + incoming
        weighted_own = reduced[0, :, :features]
        masses_own = reduced[0, :, features]
        own = (weighted_own + prior_mass * own) / (masses_own + prior_mass)[:, None]
        if iteration + 1 < ITERS:
            half_own = 0.5 * jnp.sum(own * own, axis=1)
            high = lax.reduce_precision(half_own, exponent_bits=8, mantissa_bits=7)
            rest = half_own - high
            middle = lax.reduce_precision(rest, exponent_bits=8, mantissa_bits=7)
            low = rest - middle
            block = jnp.concatenate(
                [
                    own.astype(jnp.bfloat16),
                    jnp.stack([high, middle, low], axis=1).astype(jnp.bfloat16),
                    jnp.zeros((share_rows, 125), jnp.bfloat16),
                ],
                axis=1,
            )
            on_plane = lax.all_to_all(
                jnp.broadcast_to(block[None], (plane,) + block.shape),
                PLANE,
                split_axis=0,
                concat_axis=0,
                tiled=True,
            )
            partner_plane = lax.ppermute(on_plane, "core", [(0, 1), (1, 0)])
            everyone = jnp.concatenate(
                [
                    jnp.where(core == 0, on_plane, partner_plane),
                    jnp.where(core == 0, partner_plane, on_plane),
                ],
                axis=0,
            ).reshape(K, features + 128)
            prototype_lowbits = everyone[:, :features]
            parts = everyone[:, features : features + 3].astype(jnp.float32)
            half_quadratic_length = (parts[:, 0] + parts[:, 1]) + parts[:, 2]
    own_slot = slot_of[None, :] == jnp.arange(clusters * capacity, dtype=jnp.int32)[:, None]
    row_energy = jnp.sum(jnp.where(own_slot, returned[:, None], 0.0), axis=0)
    refined = lax.ppermute(own, ("core", "yhi"), [(0, 0), (1, 2), (2, 1), (3, 3)])
    return (refined, row_energy)


def solution(mesh):
    groups, members = mesh.devices.shape
    fine = Mesh(mesh.devices.reshape(groups // 2, 2, 2, members // 8, 4), ALL)
    in_specs = (P(ALL, None), P(ALL, None), P(("z", "core"), None))
    out_specs = (P(ALL, None), P(ALL))
    return jax.shard_map(steps, mesh=fine, in_specs=in_specs, out_specs=out_specs, check_vma=False)
```

```python
import math

import jax
import jax.numpy as jnp
from jax import lax
from jax.sharding import Mesh
from jax.sharding import PartitionSpec as P


K = 512
ITERS = 2


smoothing_scale = 0.004
prior_mass = 32.0
empty_mark = 2.0


ALL = ("z", "core", "yhi", "ylo", "x")
ROUTE = ("z", "yhi", "core", "ylo", "x")
TEAM = ("core", "ylo", "x")
PLANE = ("ylo", "x")


def steps(embeddings, coarse_ids, centroid_seeds):
    rows_dev, features = embeddings.shape
    cores = lax.axis_size("core")
    plane = lax.axis_size("ylo") * lax.axis_size("x")
    members = cores * plane
    clusters = members * lax.axis_size("z") * lax.axis_size("yhi")
    capacity = 2 * rows_dev // clusters
    share_rows = K // members
    core = lax.axis_index("core")
    yhi = lax.axis_index("yhi")
    spot = lax.axis_index(PLANE)
    first_row = lax.axis_index(TEAM) * share_rows
    partner = lax.ppermute(centroid_seeds, "core", [(0, 1), (1, 0)])
    seeds16 = jnp.where(core == yhi, centroid_seeds, partner)
    widened = embeddings.astype(jnp.float32)
    unit_rows = (
        widened
        * lax.rsqrt(jnp.mean(widened * widened, axis=1, keepdims=True) + 1e-06)
        / math.sqrt(features)
    ).astype(jnp.bfloat16)
    cluster_of = coarse_ids[:, 0]
    order = jnp.arange(rows_dev, dtype=jnp.int32)
    earlier_same = (cluster_of[None, :] == cluster_of[:, None]) & (order[None, :] < order[:, None])
    row_rank = jnp.sum(earlier_same.astype(jnp.int32), axis=1)
    slot_of = cluster_of * capacity + row_rank
    placement = (
        slot_of[None, :] == jnp.arange(clusters * capacity, dtype=jnp.int32)[:, None]
    ).astype(jnp.bfloat16)
    filled = jnp.sum(placement.astype(jnp.float32), axis=1) > 0.5
    empty_row = jnp.where(
        jnp.arange(features) == 0, jnp.bfloat16(empty_mark), jnp.bfloat16(0)
    ).astype(jnp.bfloat16)
    gathered = jnp.dot(placement, unit_rows, preferred_element_type=jnp.float32).astype(
        jnp.bfloat16
    )
    packed = jnp.where(filled[:, None], gathered, empty_row[None, :])
    arrived = lax.all_to_all(packed, ROUTE, split_axis=0, concat_axis=0, tiled=True)
    slot_mask = (arrived[:, 0].astype(jnp.float32) < 1.5).astype(jnp.float32)
    widened_rows = jnp.concatenate(
        [
            arrived,
            jnp.ones((arrived.shape[0], 1), jnp.bfloat16),
            jnp.zeros((arrived.shape[0], 127), jnp.bfloat16),
        ],
        axis=1,
    )
    seeds = seeds16.astype(jnp.float32)
    own = lax.dynamic_slice_in_dim(seeds, first_row, share_rows, 0)
    prototype_lowbits = seeds16
    half_quadratic_length = 0.5 * jnp.sum(seeds * seeds, axis=1)
    for iteration in range(ITERS):
        similarity_logits = (
            jnp.dot(arrived, prototype_lowbits.T, preferred_element_type=jnp.float32)
            - half_quadratic_length[None, :]
        ) / smoothing_scale
        row_max = jnp.max(similarity_logits, axis=1, keepdims=True)
        powers = jnp.exp(similarity_logits - row_max)
        row_sum = jnp.sum(powers, axis=1, keepdims=True)
        weights = (powers / row_sum * slot_mask[:, None]).astype(jnp.bfloat16)
        closing_log_partition = row_max[:, 0] + jnp.log(row_sum[:, 0])
        if iteration + 1 == ITERS:
            returned = lax.all_to_all(
                smoothing_scale * closing_log_partition, ROUTE, split_axis=0, concat_axis=0,
                tiled=True,
            )
        if iteration + 1 < ITERS:
            weighted = jnp.einsum("rk,rd->kd", weights, arrived, preferred_element_type=jnp.float32)
            masses = jnp.sum(weights.astype(jnp.float32), axis=0)
            combined = jnp.concatenate(
                [
                    weighted.reshape(members, share_rows * features),
                    jnp.pad(masses.reshape(members, share_rows), ((0, 0), (0, 128 - share_rows))),
                ],
                axis=1,
            )
            width = combined.shape[1]
            by_core = combined.reshape(cores, plane, width)
            mine = lax.dynamic_index_in_dim(by_core, core, 0, keepdims=False)
            theirs = lax.dynamic_index_in_dim(by_core, 1 - core, 0, keepdims=False)
            halves = mine + lax.ppermute(theirs, "core", [(0, 1), (1, 0)])
            reduced = lax.dynamic_index_in_dim(halves, spot, 0, keepdims=True)
            for shift in range(1, plane):
                outgoing = lax.dynamic_index_in_dim(halves, (spot + shift) % plane, 0, keepdims=True)
                incoming = lax.ppermute(
                    outgoing, PLANE, [(i, (i + shift) % plane) for i in range(plane)]
                )
                reduced = reduced + incoming
            weighted_own = reduced[0, : share_rows * features].reshape(share_rows, features)
            masses_own = reduced[0, share_rows * features : share_rows * features + share_rows]
        else:
            weighted = jnp.einsum(
                "rk,rd->kd", weights, widened_rows, preferred_element_type=jnp.float32
            )
            by_core = weighted.reshape(cores, plane, share_rows, features + 128)
            mine = lax.dynamic_index_in_dim(by_core, core, 0, keepdims=False)
            theirs = lax.dynamic_index_in_dim(by_core, 1 - core, 0, keepdims=False)
            halves = mine + lax.ppermute(theirs, "core", [(0, 1), (1, 0)])
            reduced = lax.dynamic_index_in_dim(halves, spot, 0, keepdims=True)
            for shift in range(1, plane):
                outgoing = lax.dynamic_index_in_dim(
                    halves, (spot + shift) % plane, 0, keepdims=True
                )
                incoming = lax.ppermute(
                    outgoing, PLANE, [(i, (i + shift) % plane) for i in range(plane)]
                )
                reduced = reduced + incoming
            weighted_own = reduced[0, :, :features]
            masses_own = reduced[0, :, features]
        own = (weighted_own + prior_mass * own) / (masses_own + prior_mass)[:, None]
        if iteration + 1 < ITERS:
            half_own = 0.5 * jnp.sum(own * own, axis=1)
            high = lax.reduce_precision(half_own, exponent_bits=8, mantissa_bits=7)
            rest = half_own - high
            middle = lax.reduce_precision(rest, exponent_bits=8, mantissa_bits=7)
            low = rest - middle
            block = jnp.concatenate(
                [
                    own.astype(jnp.bfloat16),
                    jnp.stack([high, middle, low], axis=1).astype(jnp.bfloat16),
                    jnp.zeros((share_rows, 125), jnp.bfloat16),
                ],
                axis=1,
            )
            on_plane = lax.all_to_all(
                jnp.broadcast_to(block[None], (plane,) + block.shape),
                PLANE,
                split_axis=0,
                concat_axis=0,
                tiled=True,
            )
            partner_plane = lax.ppermute(on_plane, "core", [(0, 1), (1, 0)])
            everyone = jnp.concatenate(
                [
                    jnp.where(core == 0, on_plane, partner_plane),
                    jnp.where(core == 0, partner_plane, on_plane),
                ],
                axis=0,
            ).reshape(K, features + 128)
            prototype_lowbits = everyone[:, :features]
            parts = everyone[:, features : features + 3].astype(jnp.float32)
            half_quadratic_length = (parts[:, 0] + parts[:, 1]) + parts[:, 2]
    own_slot = slot_of[None, :] == jnp.arange(clusters * capacity, dtype=jnp.int32)[:, None]
    row_energy = jnp.sum(jnp.where(own_slot, returned[:, None], 0.0), axis=0)
    refined = lax.ppermute(own, ("core", "yhi"), [(0, 0), (1, 2), (2, 1), (3, 3)])
    return (refined, row_energy)


def solution(mesh):
    groups, members = mesh.devices.shape
    fine = Mesh(mesh.devices.reshape(groups // 2, 2, 2, members // 8, 4), ALL)
    in_specs = (P(ALL, None), P(ALL, None), P(("z", "core"), None))
    out_specs = (P(ALL, None), P(ALL))
    return jax.shard_map(steps, mesh=fine, in_specs=in_specs, out_specs=out_specs, check_vma=False)
```

```python
import math

import jax
import jax.numpy as jnp
from jax import lax
from jax.sharding import Mesh
from jax.sharding import PartitionSpec as P


K = 512
ITERS = 2


smoothing_scale = 0.004
prior_mass = 32.0
empty_mark = 2.0


ALL = ("z", "core", "yhi", "ylo", "x")
ROUTE = ("z", "yhi", "core", "ylo", "x")
TEAM = ("core", "ylo", "x")
PLANE = ("ylo", "x")


def steps(embeddings, coarse_ids, centroid_seeds):
    rows_dev, features = embeddings.shape
    cores = lax.axis_size("core")
    plane = lax.axis_size("ylo") * lax.axis_size("x")
    members = cores * plane
    clusters = members * lax.axis_size("z") * lax.axis_size("yhi")
    capacity = 2 * rows_dev // clusters
    share_rows = K // members
    core = lax.axis_index("core")
    yhi = lax.axis_index("yhi")
    spot = lax.axis_index(PLANE)
    first_row = lax.axis_index(TEAM) * share_rows
    partner = lax.ppermute(centroid_seeds, "core", [(0, 1), (1, 0)])
    seeds16 = jnp.where(core == yhi, centroid_seeds, partner)
    widened = embeddings.astype(jnp.float32)
    unit_rows = (
        widened
        * lax.rsqrt(jnp.mean(widened * widened, axis=1, keepdims=True) + 1e-06)
        / math.sqrt(features)
    ).astype(jnp.bfloat16)
    cluster_of = coarse_ids[:, 0]
    onehot = (cluster_of[:, None] == jnp.arange(clusters, dtype=jnp.int32)[None, :]).astype(
        jnp.int32
    )
    row_rank = jnp.sum((jnp.cumsum(onehot, axis=0) - onehot) * onehot, axis=1)
    slot_of = cluster_of * capacity + row_rank
    placement = (
        slot_of[None, :] == jnp.arange(clusters * capacity, dtype=jnp.int32)[:, None]
    ).astype(jnp.bfloat16)
    filled = jnp.sum(placement.astype(jnp.float32), axis=1) > 0.5
    empty_row = jnp.where(
        jnp.arange(features) == 0, jnp.bfloat16(empty_mark), jnp.bfloat16(0)
    ).astype(jnp.bfloat16)
    gathered = jnp.dot(placement, unit_rows, preferred_element_type=jnp.float32).astype(
        jnp.bfloat16
    )
    packed = jnp.where(filled[:, None], gathered, empty_row[None, :])
    arrived = lax.all_to_all(packed, ROUTE, split_axis=0, concat_axis=0, tiled=True)
    slot_mask = (arrived[:, 0].astype(jnp.float32) < 1.5).astype(jnp.float32)
    widened_rows = jnp.concatenate(
        [
            arrived,
            jnp.ones((arrived.shape[0], 1), jnp.bfloat16),
            jnp.zeros((arrived.shape[0], 127), jnp.bfloat16),
        ],
        axis=1,
    )
    seeds = seeds16.astype(jnp.float32)
    own = lax.dynamic_slice_in_dim(seeds, first_row, share_rows, 0)
    prototype_lowbits = seeds16
    half_quadratic_length = 0.5 * jnp.sum(seeds * seeds, axis=1)
    for iteration in range(ITERS):
        similarity_logits = (
            jnp.dot(arrived, prototype_lowbits.T, preferred_element_type=jnp.float32)
            - half_quadratic_length[None, :]
        ) / smoothing_scale
        row_max = jnp.max(similarity_logits, axis=1, keepdims=True)
        powers = jnp.exp(similarity_logits - row_max)
        row_sum = jnp.sum(powers, axis=1, keepdims=True)
        weights = (powers / row_sum * slot_mask[:, None]).astype(jnp.bfloat16)
        closing_log_partition = row_max[:, 0] + jnp.log(row_sum[:, 0])
        if iteration + 1 == ITERS:
            returned = lax.all_to_all(
                smoothing_scale * closing_log_partition, ROUTE, split_axis=0, concat_axis=0,
                tiled=True,
            )
        if iteration + 1 < ITERS:
            weighted = jnp.einsum("rk,rd->kd", weights, arrived, preferred_element_type=jnp.float32)
            masses = jnp.sum(weights.astype(jnp.float32), axis=0)
            combined = jnp.concatenate(
                [
                    weighted.reshape(members, share_rows * features),
                    jnp.pad(masses.reshape(members, share_rows), ((0, 0), (0, 128 - share_rows))),
                ],
                axis=1,
            )
            width = combined.shape[1]
            by_core = combined.reshape(cores, plane, width)
            mine = lax.dynamic_index_in_dim(by_core, core, 0, keepdims=False)
            theirs = lax.dynamic_index_in_dim(by_core, 1 - core, 0, keepdims=False)
            halves = mine + lax.ppermute(theirs, "core", [(0, 1), (1, 0)])
            reduced = lax.dynamic_index_in_dim(halves, spot, 0, keepdims=True)
            for shift in range(1, plane):
                outgoing = lax.dynamic_index_in_dim(halves, (spot + shift) % plane, 0, keepdims=True)
                incoming = lax.ppermute(
                    outgoing, PLANE, [(i, (i + shift) % plane) for i in range(plane)]
                )
                reduced = reduced + incoming
            weighted_own = reduced[0, : share_rows * features].reshape(share_rows, features)
            masses_own = reduced[0, share_rows * features : share_rows * features + share_rows]
        else:
            half_rows = K // cores

            def side_sums(side):
                picked = lax.dynamic_slice_in_dim(weights, side * half_rows, half_rows, 1)
                return jnp.einsum(
                    "rk,rd->kd", picked, widened_rows, preferred_element_type=jnp.float32
                ).reshape(plane, share_rows, features + 128)

            got = lax.ppermute(side_sums(1 - core), "core", [(0, 1), (1, 0)])
            halves = side_sums(core) + got
            reduced = lax.dynamic_index_in_dim(halves, spot, 0, keepdims=True)
            for shift in range(1, plane):
                outgoing = lax.dynamic_index_in_dim(
                    halves, (spot + shift) % plane, 0, keepdims=True
                )
                incoming = lax.ppermute(
                    outgoing, PLANE, [(i, (i + shift) % plane) for i in range(plane)]
                )
                reduced = reduced + incoming
            weighted_own = reduced[0, :, :features]
            masses_own = reduced[0, :, features]
        own = (weighted_own + prior_mass * own) / (masses_own + prior_mass)[:, None]
        if iteration + 1 < ITERS:
            half_own = 0.5 * jnp.sum(own * own, axis=1)
            high = lax.reduce_precision(half_own, exponent_bits=8, mantissa_bits=7)
            rest = half_own - high
            middle = lax.reduce_precision(rest, exponent_bits=8, mantissa_bits=7)
            low = rest - middle
            block = jnp.concatenate(
                [
                    own.astype(jnp.bfloat16),
                    jnp.stack([high, middle, low], axis=1).astype(jnp.bfloat16),
                    jnp.zeros((share_rows, 125), jnp.bfloat16),
                ],
                axis=1,
            )
            on_plane = lax.all_to_all(
                jnp.broadcast_to(block[None], (plane,) + block.shape),
                PLANE,
                split_axis=0,
                concat_axis=0,
                tiled=True,
            )
            partner_plane = lax.ppermute(on_plane, "core", [(0, 1), (1, 0)])
            everyone = jnp.concatenate(
                [
                    jnp.where(core == 0, on_plane, partner_plane),
                    jnp.where(core == 0, partner_plane, on_plane),
                ],
                axis=0,
            ).reshape(K, features + 128)
            prototype_lowbits = everyone[:, :features]
            parts = everyone[:, features : features + 3].astype(jnp.float32)
            half_quadratic_length = (parts[:, 0] + parts[:, 1]) + parts[:, 2]
    own_slot = slot_of[None, :] == jnp.arange(clusters * capacity, dtype=jnp.int32)[:, None]
    row_energy = jnp.sum(jnp.where(own_slot, returned[:, None], 0.0), axis=0)
    refined = lax.ppermute(own, ("core", "yhi"), [(0, 0), (1, 2), (2, 1), (3, 3)])
    return (refined, row_energy)


def solution(mesh):
    groups, members = mesh.devices.shape
    fine = Mesh(mesh.devices.reshape(groups // 2, 2, 2, members // 8, 4), ALL)
    in_specs = (P(ALL, None), P(ALL, None), P(("z", "core"), None))
    out_specs = (P(ALL, None), P(ALL))
    return jax.shard_map(steps, mesh=fine, in_specs=in_specs, out_specs=out_specs, check_vma=False)
```

```python
import math

import jax
import jax.numpy as jnp
from jax import lax
from jax.sharding import Mesh
from jax.sharding import PartitionSpec as P


K = 512
ITERS = 2


smoothing_scale = 0.004
prior_mass = 32.0
empty_mark = 2.0


ALL = ("z", "core", "yhi", "ylo", "x")
ROUTE = ("z", "yhi", "core", "ylo", "x")
TEAM = ("core", "ylo", "x")
PLANE = ("ylo", "x")


def steps(embeddings, coarse_ids, centroid_seeds):
    rows_dev, features = embeddings.shape
    cores = lax.axis_size("core")
    plane = lax.axis_size("ylo") * lax.axis_size("x")
    members = cores * plane
    clusters = members * lax.axis_size("z") * lax.axis_size("yhi")
    capacity = 2 * rows_dev // clusters
    share_rows = K // members
    core = lax.axis_index("core")
    yhi = lax.axis_index("yhi")
    spot = lax.axis_index(PLANE)
    first_row = lax.axis_index(TEAM) * share_rows
    partner = lax.ppermute(centroid_seeds, "core", [(0, 1), (1, 0)])
    seeds16 = jnp.where(core == yhi, centroid_seeds, partner)
    widened = embeddings.astype(jnp.float32)
    unit_rows = (
        widened
        * lax.rsqrt(jnp.mean(widened * widened, axis=1, keepdims=True) + 1e-06)
        / math.sqrt(features)
    ).astype(jnp.bfloat16)
    cluster_of = coarse_ids[:, 0]
    onehot = (cluster_of[:, None] == jnp.arange(clusters, dtype=jnp.int32)[None, :]).astype(
        jnp.int32
    )
    row_rank = jnp.sum((jnp.cumsum(onehot, axis=0) - onehot) * onehot, axis=1)
    slot_of = cluster_of * capacity + row_rank
    placement = (
        slot_of[None, :] == jnp.arange(clusters * capacity, dtype=jnp.int32)[:, None]
    ).astype(jnp.bfloat16)
    filled = jnp.sum(placement.astype(jnp.float32), axis=1) > 0.5
    empty_row = jnp.where(
        jnp.arange(features) == 0, jnp.bfloat16(empty_mark), jnp.bfloat16(0)
    ).astype(jnp.bfloat16)
    gathered = jnp.dot(placement, unit_rows, preferred_element_type=jnp.float32).astype(
        jnp.bfloat16
    )
    packed = jnp.where(filled[:, None], gathered, empty_row[None, :])
    arrived = lax.all_to_all(packed, ROUTE, split_axis=0, concat_axis=0, tiled=True)
    slot_mask = (arrived[:, 0].astype(jnp.float32) < 1.5).astype(jnp.float32)
    widened_rows = jnp.concatenate(
        [
            arrived,
            jnp.ones((arrived.shape[0], 1), jnp.bfloat16),
            jnp.zeros((arrived.shape[0], 127), jnp.bfloat16),
        ],
        axis=1,
    )
    seeds = seeds16.astype(jnp.float32)
    own = lax.dynamic_slice_in_dim(seeds, first_row, share_rows, 0)
    prototype_lowbits = seeds16
    half_quadratic_length = 0.5 * jnp.sum(seeds * seeds, axis=1)
    for iteration in range(ITERS):
        similarity_logits = (
            jnp.dot(arrived, prototype_lowbits.T, preferred_element_type=jnp.float32)
            - half_quadratic_length[None, :]
        ) / smoothing_scale
        row_max = jnp.max(similarity_logits, axis=1, keepdims=True)
        powers = jnp.exp(similarity_logits - row_max)
        row_sum = jnp.sum(powers, axis=1, keepdims=True)
        weights = (powers / row_sum * slot_mask[:, None]).astype(jnp.bfloat16)
        closing_log_partition = row_max[:, 0] + jnp.log(row_sum[:, 0])
        if iteration + 1 == ITERS:
            returned = lax.all_to_all(
                smoothing_scale * closing_log_partition, ROUTE, split_axis=0, concat_axis=0,
                tiled=True,
            )
        if iteration + 1 < ITERS:
            weighted = jnp.einsum("rk,rd->kd", weights, arrived, preferred_element_type=jnp.float32)
            masses = jnp.sum(weights.astype(jnp.float32), axis=0)
            sums = jnp.zeros((K, features + 128), jnp.float32)
            sums = lax.dynamic_update_slice(sums, weighted, (0, 0))
            sums = lax.dynamic_update_slice(sums, masses[:, None], (0, features))
            by_core = sums.reshape(cores, plane, share_rows, features + 128)
            mine = lax.dynamic_index_in_dim(by_core, core, 0, keepdims=False)
            theirs = lax.dynamic_index_in_dim(by_core, 1 - core, 0, keepdims=False)
            halves = mine + lax.ppermute(theirs, "core", [(0, 1), (1, 0)])
            reduced = lax.dynamic_index_in_dim(halves, spot, 0, keepdims=True)
            for shift in range(1, plane):
                outgoing = lax.dynamic_index_in_dim(
                    halves, (spot + shift) % plane, 0, keepdims=True
                )
                incoming = lax.ppermute(
                    outgoing, PLANE, [(i, (i + shift) % plane) for i in range(plane)]
                )
                reduced = reduced + incoming
            weighted_own = reduced[0, :, :features]
            masses_own = reduced[0, :, features]
        else:
            weighted = jnp.einsum(
                "rk,rd->kd", weights, widened_rows, preferred_element_type=jnp.float32
            )
            by_core = weighted.reshape(cores, plane, share_rows, features + 128)
            mine = lax.dynamic_index_in_dim(by_core, core, 0, keepdims=False)
            theirs = lax.dynamic_index_in_dim(by_core, 1 - core, 0, keepdims=False)
            halves = mine + lax.ppermute(theirs, "core", [(0, 1), (1, 0)])
            reduced = lax.dynamic_index_in_dim(halves, spot, 0, keepdims=True)
            for shift in range(1, plane):
                outgoing = lax.dynamic_index_in_dim(
                    halves, (spot + shift) % plane, 0, keepdims=True
                )
                incoming = lax.ppermute(
                    outgoing, PLANE, [(i, (i + shift) % plane) for i in range(plane)]
                )
                reduced = reduced + incoming
            weighted_own = reduced[0, :, :features]
            masses_own = reduced[0, :, features]
        own = (weighted_own + prior_mass * own) / (masses_own + prior_mass)[:, None]
        if iteration + 1 < ITERS:
            half_own = 0.5 * jnp.sum(own * own, axis=1)
            high = lax.reduce_precision(half_own, exponent_bits=8, mantissa_bits=7)
            rest = half_own - high
            middle = lax.reduce_precision(rest, exponent_bits=8, mantissa_bits=7)
            low = rest - middle
            block = jnp.concatenate(
                [
                    own.astype(jnp.bfloat16),
                    jnp.stack([high, middle, low], axis=1).astype(jnp.bfloat16),
                    jnp.zeros((share_rows, 125), jnp.bfloat16),
                ],
                axis=1,
            )
            on_plane = lax.all_to_all(
                jnp.broadcast_to(block[None], (plane,) + block.shape),
                PLANE,
                split_axis=0,
                concat_axis=0,
                tiled=True,
            )
            partner_plane = lax.ppermute(on_plane, "core", [(0, 1), (1, 0)])
            everyone = jnp.concatenate(
                [
                    jnp.where(core == 0, on_plane, partner_plane),
                    jnp.where(core == 0, partner_plane, on_plane),
                ],
                axis=0,
            ).reshape(K, features + 128)
            prototype_lowbits = everyone[:, :features]
            parts = everyone[:, features : features + 3].astype(jnp.float32)
            half_quadratic_length = (parts[:, 0] + parts[:, 1]) + parts[:, 2]
    own_slot = slot_of[None, :] == jnp.arange(clusters * capacity, dtype=jnp.int32)[:, None]
    row_energy = jnp.sum(jnp.where(own_slot, returned[:, None], 0.0), axis=0)
    refined = lax.ppermute(own, ("core", "yhi"), [(0, 0), (1, 2), (2, 1), (3, 3)])
    return (refined, row_energy)


def solution(mesh):
    groups, members = mesh.devices.shape
    fine = Mesh(mesh.devices.reshape(groups // 2, 2, 2, members // 8, 4), ALL)
    in_specs = (P(ALL, None), P(ALL, None), P(("z", "core"), None))
    out_specs = (P(ALL, None), P(ALL))
    return jax.shard_map(steps, mesh=fine, in_specs=in_specs, out_specs=out_specs, check_vma=False)
```

```python
import math

import jax
import jax.numpy as jnp
from jax import lax
from jax.sharding import Mesh
from jax.sharding import PartitionSpec as P


K = 512
ITERS = 2


smoothing_scale = 0.004
prior_mass = 32.0
empty_mark = 2.0


ALL = ("z", "core", "yhi", "ylo", "x")
ROUTE = ("z", "yhi", "core", "ylo", "x")
TEAM = ("core", "ylo", "x")
PLANE = ("ylo", "x")
SHIFT_ORDER = (4, 1, 7, 2, 6, 3, 5)


def steps(embeddings, coarse_ids, centroid_seeds):
    rows_dev, features = embeddings.shape
    cores = lax.axis_size("core")
    plane = lax.axis_size("ylo") * lax.axis_size("x")
    members = cores * plane
    clusters = members * lax.axis_size("z") * lax.axis_size("yhi")
    capacity = 2 * rows_dev // clusters
    share_rows = K // members
    core = lax.axis_index("core")
    yhi = lax.axis_index("yhi")
    spot = lax.axis_index(PLANE)
    first_row = lax.axis_index(TEAM) * share_rows
    partner = lax.ppermute(centroid_seeds, "core", [(0, 1), (1, 0)])
    seeds16 = jnp.where(core == yhi, centroid_seeds, partner)
    widened = embeddings.astype(jnp.float32)
    unit_rows = (
        widened
        * lax.rsqrt(jnp.mean(widened * widened, axis=1, keepdims=True) + 1e-06)
        / math.sqrt(features)
    ).astype(jnp.bfloat16)
    cluster_of = coarse_ids[:, 0]
    onehot = (cluster_of[:, None] == jnp.arange(clusters, dtype=jnp.int32)[None, :]).astype(
        jnp.int32
    )
    row_rank = jnp.sum((jnp.cumsum(onehot, axis=0) - onehot) * onehot, axis=1)
    slot_of = cluster_of * capacity + row_rank
    placement = (
        slot_of[None, :] == jnp.arange(clusters * capacity, dtype=jnp.int32)[:, None]
    ).astype(jnp.bfloat16)
    filled = jnp.sum(placement.astype(jnp.float32), axis=1) > 0.5
    empty_row = jnp.where(
        jnp.arange(features) == 0, jnp.bfloat16(empty_mark), jnp.bfloat16(0)
    ).astype(jnp.bfloat16)
    gathered = jnp.dot(placement, unit_rows, preferred_element_type=jnp.float32).astype(
        jnp.bfloat16
    )
    packed = jnp.where(filled[:, None], gathered, empty_row[None, :])
    arrived = lax.all_to_all(packed, ROUTE, split_axis=0, concat_axis=0, tiled=True)
    slot_mask = (arrived[:, 0].astype(jnp.float32) < 1.5).astype(jnp.float32)
    widened_rows = jnp.concatenate(
        [
            arrived,
            jnp.ones((arrived.shape[0], 1), jnp.bfloat16),
            jnp.zeros((arrived.shape[0], 127), jnp.bfloat16),
        ],
        axis=1,
    )
    seeds = seeds16.astype(jnp.float32)
    own = lax.dynamic_slice_in_dim(seeds, first_row, share_rows, 0)
    prototype_lowbits = seeds16
    half_quadratic_length = 0.5 * jnp.sum(seeds * seeds, axis=1)
    for iteration in range(ITERS):
        similarity_logits = (
            jnp.dot(arrived, prototype_lowbits.T, preferred_element_type=jnp.float32)
            - half_quadratic_length[None, :]
        ) / smoothing_scale
        row_max = jnp.max(similarity_logits, axis=1, keepdims=True)
        powers = jnp.exp(similarity_logits - row_max)
        row_sum = jnp.sum(powers, axis=1, keepdims=True)
        weights = (powers / row_sum * slot_mask[:, None]).astype(jnp.bfloat16)
        closing_log_partition = row_max[:, 0] + jnp.log(row_sum[:, 0])
        if iteration + 1 == ITERS:
            returned = lax.all_to_all(
                smoothing_scale * closing_log_partition, ROUTE, split_axis=0, concat_axis=0,
                tiled=True,
            )
        if iteration + 1 < ITERS:
            weighted = jnp.einsum("rk,rd->kd", weights, arrived, preferred_element_type=jnp.float32)
            masses = jnp.sum(weights.astype(jnp.float32), axis=0)
            combined = jnp.concatenate(
                [
                    weighted.reshape(members, share_rows * features),
                    jnp.pad(masses.reshape(members, share_rows), ((0, 0), (0, 128 - share_rows))),
                ],
                axis=1,
            )
            width = combined.shape[1]
            by_core = combined.reshape(cores, plane, width)
            mine = lax.dynamic_index_in_dim(by_core, core, 0, keepdims=False)
            theirs = lax.dynamic_index_in_dim(by_core, 1 - core, 0, keepdims=False)
            halves = mine + lax.ppermute(theirs, "core", [(0, 1), (1, 0)])
            reduced = lax.dynamic_index_in_dim(halves, spot, 0, keepdims=True)
            for shift in SHIFT_ORDER:
                outgoing = lax.dynamic_index_in_dim(halves, (spot + shift) % plane, 0, keepdims=True)
                incoming = lax.ppermute(
                    outgoing, PLANE, [(i, (i + shift) % plane) for i in range(plane)]
                )
                reduced = reduced + incoming
            weighted_own = reduced[0, : share_rows * features].reshape(share_rows, features)
            masses_own = reduced[0, share_rows * features : share_rows * features + share_rows]
        else:
            weighted = jnp.einsum(
                "rk,rd->kd", weights, widened_rows, preferred_element_type=jnp.float32
            )
            by_core = weighted.reshape(cores, plane, share_rows, features + 128)
            mine = lax.dynamic_index_in_dim(by_core, core, 0, keepdims=False)
            theirs = lax.dynamic_index_in_dim(by_core, 1 - core, 0, keepdims=False)
            halves = mine + lax.ppermute(theirs, "core", [(0, 1), (1, 0)])
            reduced = lax.dynamic_index_in_dim(halves, spot, 0, keepdims=True)
            for shift in SHIFT_ORDER:
                outgoing = lax.dynamic_index_in_dim(
                    halves, (spot + shift) % plane, 0, keepdims=True
                )
                incoming = lax.ppermute(
                    outgoing, PLANE, [(i, (i + shift) % plane) for i in range(plane)]
                )
                reduced = reduced + incoming
            weighted_own = reduced[0, :, :features]
            masses_own = reduced[0, :, features]
        own = (weighted_own + prior_mass * own) / (masses_own + prior_mass)[:, None]
        if iteration + 1 < ITERS:
            half_own = 0.5 * jnp.sum(own * own, axis=1)
            high = lax.reduce_precision(half_own, exponent_bits=8, mantissa_bits=7)
            rest = half_own - high
            middle = lax.reduce_precision(rest, exponent_bits=8, mantissa_bits=7)
            low = rest - middle
            block = jnp.concatenate(
                [
                    own.astype(jnp.bfloat16),
                    jnp.stack([high, middle, low], axis=1).astype(jnp.bfloat16),
                    jnp.zeros((share_rows, 125), jnp.bfloat16),
                ],
                axis=1,
            )
            on_plane = lax.all_to_all(
                jnp.broadcast_to(block[None], (plane,) + block.shape),
                PLANE,
                split_axis=0,
                concat_axis=0,
                tiled=True,
            )
            partner_plane = lax.ppermute(on_plane, "core", [(0, 1), (1, 0)])
            everyone = jnp.concatenate(
                [
                    jnp.where(core == 0, on_plane, partner_plane),
                    jnp.where(core == 0, partner_plane, on_plane),
                ],
                axis=0,
            ).reshape(K, features + 128)
            prototype_lowbits = everyone[:, :features]
            parts = everyone[:, features : features + 3].astype(jnp.float32)
            half_quadratic_length = (parts[:, 0] + parts[:, 1]) + parts[:, 2]
    own_slot = slot_of[None, :] == jnp.arange(clusters * capacity, dtype=jnp.int32)[:, None]
    row_energy = jnp.sum(jnp.where(own_slot, returned[:, None], 0.0), axis=0)
    refined = lax.ppermute(own, ("core", "yhi"), [(0, 0), (1, 2), (2, 1), (3, 3)])
    return (refined, row_energy)


def solution(mesh):
    groups, members = mesh.devices.shape
    fine = Mesh(mesh.devices.reshape(groups // 2, 2, 2, members // 8, 4), ALL)
    in_specs = (P(ALL, None), P(ALL, None), P(("z", "core"), None))
    out_specs = (P(ALL, None), P(ALL))
    return jax.shard_map(steps, mesh=fine, in_specs=in_specs, out_specs=out_specs, check_vma=False)
```

```python
import math

import jax
import jax.numpy as jnp
from jax import lax
from jax.sharding import Mesh
from jax.sharding import PartitionSpec as P


K = 512
ITERS = 2


smoothing_scale = 0.004
prior_mass = 32.0
empty_mark = 2.0


ALL = ("z", "core", "yhi", "ylo", "x")
ROUTE = ("z", "yhi", "core", "ylo", "x")
TEAM = ("core", "ylo", "x")
PLANE = ("ylo", "x")


def steps(embeddings, coarse_ids, centroid_seeds):
    rows_dev, features = embeddings.shape
    cores = lax.axis_size("core")
    plane = lax.axis_size("ylo") * lax.axis_size("x")
    members = cores * plane
    clusters = members * lax.axis_size("z") * lax.axis_size("yhi")
    capacity = 2 * rows_dev // clusters
    share_rows = K // members
    core = lax.axis_index("core")
    yhi = lax.axis_index("yhi")
    spot = lax.axis_index(PLANE)
    first_row = lax.axis_index(TEAM) * share_rows
    partner = lax.ppermute(centroid_seeds, "core", [(0, 1), (1, 0)])
    seeds16 = jnp.where(core == yhi, centroid_seeds, partner)
    widened = embeddings.astype(jnp.float32)
    unit_rows = (
        widened
        * lax.rsqrt(jnp.mean(widened * widened, axis=1, keepdims=True) + 1e-06)
        / math.sqrt(features)
    ).astype(jnp.bfloat16)
    cluster_of = coarse_ids[:, 0]
    onehot = (cluster_of[:, None] == jnp.arange(clusters, dtype=jnp.int32)[None, :]).astype(
        jnp.int32
    )
    row_rank = jnp.sum((jnp.cumsum(onehot, axis=0) - onehot) * onehot, axis=1)
    slot_of = cluster_of * capacity + row_rank
    placement = (
        slot_of[None, :] == jnp.arange(clusters * capacity, dtype=jnp.int32)[:, None]
    ).astype(jnp.bfloat16)
    filled = jnp.sum(placement.astype(jnp.float32), axis=1) > 0.5
    empty_row = jnp.where(
        jnp.arange(features) == 0, jnp.bfloat16(empty_mark), jnp.bfloat16(0)
    ).astype(jnp.bfloat16)
    gathered = jnp.dot(placement, unit_rows, preferred_element_type=jnp.float32).astype(
        jnp.bfloat16
    )
    packed = jnp.where(filled[:, None], gathered, empty_row[None, :])
    arrived = lax.all_to_all(packed, ROUTE, split_axis=0, concat_axis=0, tiled=True)
    slot_mask = (arrived[:, 0].astype(jnp.float32) < 1.5).astype(jnp.float32)
    widened_rows = jnp.concatenate(
        [
            arrived,
            jnp.ones((arrived.shape[0], 1), jnp.bfloat16),
            jnp.zeros((arrived.shape[0], 127), jnp.bfloat16),
        ],
        axis=1,
    )
    seeds = seeds16.astype(jnp.float32)
    own = lax.dynamic_slice_in_dim(seeds, first_row, share_rows, 0)
    prototype_lowbits = seeds16
    half_quadratic_length = 0.5 * jnp.sum(seeds * seeds, axis=1)
    for iteration in range(ITERS):
        similarity_logits = (
            jnp.dot(arrived, prototype_lowbits.T, preferred_element_type=jnp.float32)
            - half_quadratic_length[None, :]
        ) / smoothing_scale
        row_max = jnp.max(similarity_logits, axis=1, keepdims=True)
        powers = jnp.exp(similarity_logits - row_max)
        row_sum = jnp.sum(powers, axis=1, keepdims=True)
        weights = (powers / row_sum * slot_mask[:, None]).astype(jnp.bfloat16)
        closing_log_partition = row_max[:, 0] + jnp.log(row_sum[:, 0])
        if iteration + 1 == ITERS:
            returned = lax.all_to_all(
                smoothing_scale * closing_log_partition, ROUTE, split_axis=0, concat_axis=0,
                tiled=True,
            )
        if iteration + 1 < ITERS:
            weighted = jnp.einsum("rk,rd->kd", weights, arrived, preferred_element_type=jnp.float32)
            masses = jnp.sum(weights.astype(jnp.float32), axis=0)
            combined = jnp.concatenate(
                [
                    weighted.reshape(members, share_rows * features),
                    jnp.pad(masses.reshape(members, share_rows), ((0, 0), (0, 128 - share_rows))),
                ],
                axis=1,
            )
            width = combined.shape[1]
            by_core = combined.reshape(cores, plane, width)
            mine = lax.dynamic_index_in_dim(by_core, core, 0, keepdims=False)
            theirs = lax.dynamic_index_in_dim(by_core, 1 - core, 0, keepdims=False)
            halves = mine + lax.ppermute(theirs, "core", [(0, 1), (1, 0)])
            reduced = lax.dynamic_index_in_dim(halves, spot, 0, keepdims=True)
            for shift in range(1, plane):
                outgoing = lax.dynamic_index_in_dim(halves, (spot + shift) % plane, 0, keepdims=True)
                incoming = lax.ppermute(
                    outgoing, PLANE, [(i, (i + shift) % plane) for i in range(plane)]
                )
                reduced = reduced + incoming
            weighted_own = reduced[0, : share_rows * features].reshape(share_rows, features)
            masses_own = reduced[0, share_rows * features : share_rows * features + share_rows]
        else:
            weighted = jnp.einsum(
                "rk,rd->kd", weights, widened_rows, preferred_element_type=jnp.float32
            )
            by_core = weighted.reshape(cores, plane, share_rows, features + 128)
            mine = by_core[0]
            theirs = by_core[1]
            halves = mine + lax.ppermute(theirs, "core", [(0, 1), (1, 0)])
            reduced = lax.dynamic_index_in_dim(halves, spot, 0, keepdims=True)
            for shift in range(1, plane):
                outgoing = lax.dynamic_index_in_dim(
                    halves, (spot + shift) % plane, 0, keepdims=True
                )
                incoming = lax.ppermute(
                    outgoing, PLANE, [(i, (i + shift) % plane) for i in range(plane)]
                )
                reduced = reduced + incoming
            weighted_own = reduced[0, :, :features]
            masses_own = reduced[0, :, features]
        own = (weighted_own + prior_mass * own) / (masses_own + prior_mass)[:, None]
        if iteration + 1 < ITERS:
            half_own = 0.5 * jnp.sum(own * own, axis=1)
            high = lax.reduce_precision(half_own, exponent_bits=8, mantissa_bits=7)
            rest = half_own - high
            middle = lax.reduce_precision(rest, exponent_bits=8, mantissa_bits=7)
            low = rest - middle
            block = jnp.concatenate(
                [
                    own.astype(jnp.bfloat16),
                    jnp.stack([high, middle, low], axis=1).astype(jnp.bfloat16),
                    jnp.zeros((share_rows, 125), jnp.bfloat16),
                ],
                axis=1,
            )
            on_plane = lax.all_to_all(
                jnp.broadcast_to(block[None], (plane,) + block.shape),
                PLANE,
                split_axis=0,
                concat_axis=0,
                tiled=True,
            )
            partner_plane = lax.ppermute(on_plane, "core", [(0, 1), (1, 0)])
            everyone = jnp.concatenate([on_plane, partner_plane], axis=0).reshape(
                K, features + 128
            )
            prototype_lowbits = everyone[:, :features]
            parts = everyone[:, features : features + 3].astype(jnp.float32)
            half_quadratic_length = (parts[:, 0] + parts[:, 1]) + parts[:, 2]
    own_slot = slot_of[None, :] == jnp.arange(clusters * capacity, dtype=jnp.int32)[:, None]
    row_energy = jnp.sum(jnp.where(own_slot, returned[:, None], 0.0), axis=0)
    refined = lax.ppermute(own, ("core", "yhi"), [(0, 0), (1, 2), (2, 1), (3, 3)])
    return (refined, row_energy)


def solution(mesh):
    groups, members = mesh.devices.shape
    fine = Mesh(mesh.devices.reshape(groups // 2, 2, 2, members // 8, 4), ALL)
    in_specs = (P(ALL, None), P(ALL, None), P(("z", "core"), None))
    out_specs = (P(ALL, None), P(ALL))
    return jax.shard_map(steps, mesh=fine, in_specs=in_specs, out_specs=out_specs, check_vma=False)
```

```python
import math

import jax
import jax.numpy as jnp
from jax import lax
from jax.sharding import Mesh
from jax.sharding import PartitionSpec as P


K = 512
ITERS = 2


smoothing_scale = 0.004
prior_mass = 32.0
empty_mark = 2.0


ALL = ("z", "core", "yhi", "ylo", "x")
ROUTE = ("z", "yhi", "core", "ylo", "x")
TEAM = ("core", "ylo", "x")
PLANE = ("ylo", "x")


def steps(embeddings, coarse_ids, centroid_seeds):
    rows_dev, features = embeddings.shape
    cores = lax.axis_size("core")
    plane = lax.axis_size("ylo") * lax.axis_size("x")
    members = cores * plane
    clusters = members * lax.axis_size("z") * lax.axis_size("yhi")
    capacity = 2 * rows_dev // clusters
    share_rows = K // members
    core = lax.axis_index("core")
    yhi = lax.axis_index("yhi")
    spot = lax.axis_index(PLANE)
    first_row = lax.axis_index(TEAM) * share_rows
    partner = lax.ppermute(centroid_seeds, "core", [(0, 1), (1, 0)])
    seeds16 = jnp.where(core == yhi, centroid_seeds, partner)
    widened = embeddings.astype(jnp.float32)
    unit_rows = (
        widened
        * lax.rsqrt(jnp.mean(widened * widened, axis=1, keepdims=True) + 1e-06)
        / math.sqrt(features)
    ).astype(jnp.bfloat16)
    cluster_of = coarse_ids[:, 0]
    onehot = (cluster_of[:, None] == jnp.arange(clusters, dtype=jnp.int32)[None, :]).astype(
        jnp.int32
    )
    row_rank = jnp.sum((jnp.cumsum(onehot, axis=0) - onehot) * onehot, axis=1)
    slot_of = cluster_of * capacity + row_rank
    placement = (
        slot_of[None, :] == jnp.arange(clusters * capacity, dtype=jnp.int32)[:, None]
    ).astype(jnp.bfloat16)
    filled = jnp.sum(placement.astype(jnp.float32), axis=1) > 0.5
    empty_row = jnp.where(
        jnp.arange(features) == 0, jnp.bfloat16(empty_mark), jnp.bfloat16(0)
    ).astype(jnp.bfloat16)
    gathered = jnp.dot(placement, unit_rows, preferred_element_type=jnp.float32).astype(
        jnp.bfloat16
    )
    packed = jnp.where(filled[:, None], gathered, empty_row[None, :])
    arrived = lax.all_to_all(packed, ROUTE, split_axis=0, concat_axis=0, tiled=True)
    slot_mask = (arrived[:, 0].astype(jnp.float32) < 1.5).astype(jnp.float32)
    widened_rows = jnp.concatenate(
        [
            arrived,
            jnp.ones((arrived.shape[0], 1), jnp.bfloat16),
            jnp.zeros((arrived.shape[0], 127), jnp.bfloat16),
        ],
        axis=1,
    )
    seeds = seeds16.astype(jnp.float32)
    own = lax.dynamic_slice_in_dim(seeds, first_row, share_rows, 0)
    prototype_lowbits = seeds16
    half_quadratic_length = 0.5 * jnp.sum(seeds * seeds, axis=1)
    for iteration in range(ITERS):
        similarity_logits = (
            jnp.dot(arrived, prototype_lowbits.T, preferred_element_type=jnp.float32)
            - half_quadratic_length[None, :]
        ) / smoothing_scale
        row_max = jnp.max(similarity_logits, axis=1, keepdims=True)
        powers = jnp.exp(similarity_logits - row_max)
        row_sum = jnp.sum(powers, axis=1, keepdims=True)
        weights = (powers / row_sum * slot_mask[:, None]).astype(jnp.bfloat16)
        closing_log_partition = row_max[:, 0] + jnp.log(row_sum[:, 0])
        if iteration + 1 == ITERS:
            returned = lax.all_to_all(
                smoothing_scale * closing_log_partition, ROUTE, split_axis=0, concat_axis=0,
                tiled=True,
            )
        if iteration + 1 < ITERS:
            weighted = jnp.einsum("rk,rd->kd", weights, arrived, preferred_element_type=jnp.float32)
            masses = jnp.sum(weights.astype(jnp.float32), axis=0)
            combined = jnp.concatenate(
                [
                    weighted.reshape(members, share_rows * features),
                    jnp.pad(masses.reshape(members, share_rows), ((0, 0), (0, 128 - share_rows))),
                ],
                axis=1,
            )
            width = combined.shape[1]
            by_core = combined.reshape(cores, plane, width)
            mine = lax.dynamic_index_in_dim(by_core, core, 0, keepdims=False)
            theirs = lax.dynamic_index_in_dim(by_core, 1 - core, 0, keepdims=False)
            halves = mine + lax.ppermute(theirs, "core", [(0, 1), (1, 0)])
            reduced = lax.dynamic_index_in_dim(halves, spot, 0, keepdims=True)
            for shift in range(1, plane):
                outgoing = lax.dynamic_index_in_dim(halves, (spot + shift) % plane, 0, keepdims=True)
                incoming = lax.ppermute(
                    outgoing, PLANE, [(i, (i + shift) % plane) for i in range(plane)]
                )
                reduced = reduced + incoming
            weighted_own = reduced[0, : share_rows * features].reshape(share_rows, features)
            masses_own = reduced[0, share_rows * features : share_rows * features + share_rows]
        else:
            weighted = jnp.einsum(
                "rk,rd->kd", weights, widened_rows, preferred_element_type=jnp.float32
            )
            by_core = weighted.reshape(cores, plane, share_rows, features + 128)
            mine = lax.dynamic_index_in_dim(by_core, core, 0, keepdims=False)
            theirs = lax.dynamic_index_in_dim(by_core, 1 - core, 0, keepdims=False)
            halves = mine + lax.ppermute(theirs, "core", [(0, 1), (1, 0)])
            reduced = lax.dynamic_index_in_dim(halves, spot, 0, keepdims=True)
            for shift in range(1, plane):
                outgoing = lax.dynamic_index_in_dim(
                    halves, (spot + shift) % plane, 0, keepdims=True
                )
                incoming = lax.ppermute(
                    outgoing, PLANE, [(i, (i + shift) % plane) for i in range(plane)]
                )
                reduced = reduced + incoming
            weighted_own = reduced[0, :, :features]
            masses_own = reduced[0, :, features]
        own = (weighted_own + prior_mass * own) / (masses_own + prior_mass)[:, None]
        if iteration + 1 < ITERS:
            half_own = 0.5 * jnp.sum(own * own, axis=1)
            high = lax.reduce_precision(half_own, exponent_bits=8, mantissa_bits=7)
            rest = half_own - high
            middle = lax.reduce_precision(rest, exponent_bits=8, mantissa_bits=7)
            low = rest - middle
            block = jnp.concatenate(
                [
                    own.astype(jnp.bfloat16),
                    jnp.stack([high, middle, low], axis=1).astype(jnp.bfloat16),
                    jnp.zeros((share_rows, 125), jnp.bfloat16),
                ],
                axis=1,
            )
            on_plane = lax.all_to_all(
                jnp.broadcast_to(block[None], (plane,) + block.shape),
                PLANE,
                split_axis=0,
                concat_axis=0,
                tiled=True,
            )
            partner_plane = lax.ppermute(on_plane, "core", [(0, 1), (1, 0)])
            everyone = jnp.concatenate(
                [
                    jnp.where(core == 0, on_plane, partner_plane),
                    jnp.where(core == 0, partner_plane, on_plane),
                ],
                axis=0,
            ).reshape(K, features + 128)
            prototype_lowbits = everyone[:, :features]
            parts = everyone[:, features : features + 3].astype(jnp.float32)
            half_quadratic_length = (parts[:, 0] + parts[:, 1]) + parts[:, 2]
    own_slot = slot_of[None, :] == jnp.arange(clusters * capacity, dtype=jnp.int32)[:, None]
    row_energy = jnp.sum(jnp.where(own_slot, returned[:, None], 0.0), axis=0)
    refined = lax.ppermute(own, ("core", "yhi"), [(0, 0), (1, 2), (2, 1), (3, 3)])
    return (refined, row_energy)


def solution(mesh):
    groups, members = mesh.devices.shape
    fine = Mesh(mesh.devices.reshape(groups // 2, 2, 2, members // 8, 4), ALL)
    in_specs = (P(ALL, None), P(ALL, None), P(("z", "core"), None))
    out_specs = (P(ALL, None), P(ALL))
    return jax.shard_map(steps, mesh=fine, in_specs=in_specs, out_specs=out_specs, check_vma=False)
```

```python
import math

import jax
import jax.numpy as jnp
from jax import lax
from jax.sharding import Mesh
from jax.sharding import PartitionSpec as P


K = 512
ITERS = 2


smoothing_scale = 0.004
prior_mass = 32.0
empty_mark = 2.0


ALL = ("z", "core", "yhi", "ylo", "x")
ROUTE = ("z", "yhi", "core", "ylo", "x")
TEAM = ("core", "ylo", "x")
PLANE = ("ylo", "x")


def steps(embeddings, coarse_ids, centroid_seeds):
    rows_dev, features = embeddings.shape
    cores = lax.axis_size("core")
    plane = lax.axis_size("ylo") * lax.axis_size("x")
    members = cores * plane
    clusters = members * lax.axis_size("z") * lax.axis_size("yhi")
    capacity = 2 * rows_dev // clusters
    share_rows = K // members
    core = lax.axis_index("core")
    yhi = lax.axis_index("yhi")
    spot = lax.axis_index(PLANE)
    first_row = lax.axis_index(TEAM) * share_rows
    partner = lax.ppermute(centroid_seeds, "core", [(0, 1), (1, 0)])
    seeds16 = jnp.where(core == yhi, centroid_seeds, partner)
    widened = embeddings.astype(jnp.float32)
    unit_rows = (
        widened
        * lax.rsqrt(jnp.mean(widened * widened, axis=1, keepdims=True) + 1e-06)
        / math.sqrt(features)
    ).astype(jnp.bfloat16)
    cluster_of = coarse_ids[:, 0]
    onehot = (cluster_of[:, None] == jnp.arange(clusters, dtype=jnp.int32)[None, :]).astype(
        jnp.int32
    )
    row_rank = jnp.sum((jnp.cumsum(onehot, axis=0) - onehot) * onehot, axis=1)
    slot_of = cluster_of * capacity + row_rank
    placement = (
        slot_of[None, :] == jnp.arange(clusters * capacity, dtype=jnp.int32)[:, None]
    ).astype(jnp.bfloat16)
    filled = jnp.sum(placement.astype(jnp.float32), axis=1) > 0.5
    empty_row = jnp.where(
        jnp.arange(features) == 0, jnp.bfloat16(empty_mark), jnp.bfloat16(0)
    ).astype(jnp.bfloat16)
    gathered = jnp.dot(placement, unit_rows, preferred_element_type=jnp.float32).astype(
        jnp.bfloat16
    )
    packed = jnp.where(filled[:, None], gathered, empty_row[None, :])
    arrived = lax.all_to_all(packed, ROUTE, split_axis=0, concat_axis=0, tiled=True)
    slot_mask = (arrived[:, 0].astype(jnp.float32) < 1.5).astype(jnp.float32)
    widened_rows = jnp.concatenate(
        [
            arrived,
            jnp.ones((arrived.shape[0], 1), jnp.bfloat16),
            jnp.zeros((arrived.shape[0], 127), jnp.bfloat16),
        ],
        axis=1,
    )
    seeds = seeds16.astype(jnp.float32)
    own = lax.dynamic_slice_in_dim(seeds, first_row, share_rows, 0)
    prototype_lowbits = seeds16
    half_quadratic_length = 0.5 * jnp.sum(seeds * seeds, axis=1)
    for iteration in range(ITERS):
        similarity_logits = (
            jnp.dot(arrived, prototype_lowbits.T, preferred_element_type=jnp.float32)
            - half_quadratic_length[None, :]
        ) / smoothing_scale
        row_max = jnp.max(similarity_logits, axis=1, keepdims=True)
        powers = jnp.exp(similarity_logits - row_max)
        row_sum = jnp.sum(powers, axis=1, keepdims=True)
        weights = (powers / row_sum * slot_mask[:, None]).astype(jnp.bfloat16)
        closing_log_partition = row_max[:, 0] + jnp.log(row_sum[:, 0])
        if iteration + 1 == ITERS:
            returned = lax.all_to_all(
                smoothing_scale * closing_log_partition, ROUTE, split_axis=0, concat_axis=0,
                tiled=True,
            )
        if iteration + 1 < ITERS:
            weighted = jnp.einsum("rk,rd->kd", weights, arrived, preferred_element_type=jnp.float32)
            masses = jnp.dot(
                jnp.ones((1, weights.shape[0]), jnp.bfloat16), weights,
                preferred_element_type=jnp.float32,
            )[0]
            combined = jnp.concatenate(
                [
                    weighted.reshape(members, share_rows * features),
                    jnp.pad(masses.reshape(members, share_rows), ((0, 0), (0, 128 - share_rows))),
                ],
                axis=1,
            )
            width = combined.shape[1]
            by_core = combined.reshape(cores, plane, width)
            mine = lax.dynamic_index_in_dim(by_core, core, 0, keepdims=False)
            theirs = lax.dynamic_index_in_dim(by_core, 1 - core, 0, keepdims=False)
            halves = mine + lax.ppermute(theirs, "core", [(0, 1), (1, 0)])
            reduced = lax.dynamic_index_in_dim(halves, spot, 0, keepdims=True)
            for shift in range(1, plane):
                outgoing = lax.dynamic_index_in_dim(halves, (spot + shift) % plane, 0, keepdims=True)
                incoming = lax.ppermute(
                    outgoing, PLANE, [(i, (i + shift) % plane) for i in range(plane)]
                )
                reduced = reduced + incoming
            weighted_own = reduced[0, : share_rows * features].reshape(share_rows, features)
            masses_own = reduced[0, share_rows * features : share_rows * features + share_rows]
        else:
            weighted = jnp.einsum(
                "rk,rd->kd", weights, widened_rows, preferred_element_type=jnp.float32
            )
            by_core = weighted.reshape(cores, plane, share_rows, features + 128)
            mine = lax.dynamic_index_in_dim(by_core, core, 0, keepdims=False)
            theirs = lax.dynamic_index_in_dim(by_core, 1 - core, 0, keepdims=False)
            halves = mine + lax.ppermute(theirs, "core", [(0, 1), (1, 0)])
            reduced = lax.dynamic_index_in_dim(halves, spot, 0, keepdims=True)
            for shift in range(1, plane):
                outgoing = lax.dynamic_index_in_dim(
                    halves, (spot + shift) % plane, 0, keepdims=True
                )
                incoming = lax.ppermute(
                    outgoing, PLANE, [(i, (i + shift) % plane) for i in range(plane)]
                )
                reduced = reduced + incoming
            weighted_own = reduced[0, :, :features]
            masses_own = reduced[0, :, features]
        own = (weighted_own + prior_mass * own) / (masses_own + prior_mass)[:, None]
        if iteration + 1 < ITERS:
            half_own = 0.5 * jnp.sum(own * own, axis=1)
            high = lax.reduce_precision(half_own, exponent_bits=8, mantissa_bits=7)
            rest = half_own - high
            middle = lax.reduce_precision(rest, exponent_bits=8, mantissa_bits=7)
            low = rest - middle
            block = jnp.concatenate(
                [
                    own.astype(jnp.bfloat16),
                    jnp.stack([high, middle, low], axis=1).astype(jnp.bfloat16),
                    jnp.zeros((share_rows, 125), jnp.bfloat16),
                ],
                axis=1,
            )
            on_plane = lax.all_to_all(
                jnp.broadcast_to(block[None], (plane,) + block.shape),
                PLANE,
                split_axis=0,
                concat_axis=0,
                tiled=True,
            )
            partner_plane = lax.ppermute(on_plane, "core", [(0, 1), (1, 0)])
            everyone = jnp.concatenate(
                [
                    jnp.where(core == 0, on_plane, partner_plane),
                    jnp.where(core == 0, partner_plane, on_plane),
                ],
                axis=0,
            ).reshape(K, features + 128)
            prototype_lowbits = everyone[:, :features]
            parts = everyone[:, features : features + 3].astype(jnp.float32)
            half_quadratic_length = (parts[:, 0] + parts[:, 1]) + parts[:, 2]
    own_slot = slot_of[None, :] == jnp.arange(clusters * capacity, dtype=jnp.int32)[:, None]
    row_energy = jnp.sum(jnp.where(own_slot, returned[:, None], 0.0), axis=0)
    refined = lax.ppermute(own, ("core", "yhi"), [(0, 0), (1, 2), (2, 1), (3, 3)])
    return (refined, row_energy)


def solution(mesh):
    groups, members = mesh.devices.shape
    fine = Mesh(mesh.devices.reshape(groups // 2, 2, 2, members // 8, 4), ALL)
    in_specs = (P(ALL, None), P(ALL, None), P(("z", "core"), None))
    out_specs = (P(ALL, None), P(ALL))
    return jax.shard_map(steps, mesh=fine, in_specs=in_specs, out_specs=out_specs, check_vma=False)
```
